32 devices in a mesh: dp: 4 (over z), pipe: 2 (over core), expert: 4 (over y, x).
Axes of the slice: x: 2, y: 2, z: 4, core: 2. Of those that a mesh axis runs over, the one named last changes fastest.
Arguments:
- tokens: bfloat16 [2, 96, 3072], P(None, 'expert'), may hold values from -6 to 6
- expert_ids: int32 [2, 2, 96, 2], P('pipe', None, 'expert'), may hold values from 0 to 3, all different within a row; in each aligned block of 24 rows (0 to 23, 24 to 47, ..., all dimensions but the last counted through in order) at most 16 rows name the same one
- gates: float32 [2, 2, 96, 2], P('pipe', None, 'expert'), may hold values from 0.1 to 1
- w_gate: bfloat16 [2, 4, 3072, 704], P('pipe', 'expert', None, 'dp'), may hold values from -0.109375 to 0.109375
- w_up: bfloat16 [2, 4, 3072, 704], P('pipe', 'expert', None, 'dp'), may hold values from -0.109375 to 0.109375
- w_down: bfloat16 [2, 4, 704, 3072], P('pipe', 'expert', 'dp'), may hold values from -0.3125 to 0.3125
Outputs:
- layer_out: bfloat16 [2, 2, 96, 3072], P('pipe', None, 'expert', 'dp')
The draws below stay inside these ranges and needn't reach their ends.
Inputs may be any that keep to these rules, and one draw needn't show every extreme that they name: `expert_ids`: each token names 2 different experts in each layer. Among the tokens of one index of expert in one layer and micro-batch (aligned blocks of 24 tokens) no expert is named by more than 16 tokens, and in some block an expert is named by exactly 16.
All inputs are finite; a program needn't handle non-finite values.
Results may differ from the reference program's by a relative error of at most 0.0052.
Values may be sent and summed in bfloat16 or wider, within the bound.
No kernel may reach another device: no remote copies, remote signals or barrier semaphores. Data moves between devices by JAX's collectives and lax.ppermute only.
A program may use at most 64 MiB of HBM per device.

```python
import math
import jax
import jax.numpy as jnp
import numpy as np
from jax import lax

D = 3072
TOP = 2
CAP = 16
MICRO = 2
LAYERS = 2
EXPERTS = 4
FF = 704
TOK_DEV = 24
TOKENS = 96


def strengthened(array, own_key, source, target, shards_of, factor):
    def block_of(position):
        return (jnp.arange(array.shape[position]) // (array.shape[position] // shards_of)).reshape((-1,) + (1,) * (array.ndim - 1 - position))

    one_side = jax.random.permutation(own_key, shards_of)[block_of(target)]
    second = (block_of(target) + shards_of // 2) % shards_of
    return jnp.where((block_of(source) == one_side) | (block_of(source) == second), factor * array, array)


def block_scale(key, dims, pieces, smallest, high):
    gain, own = 1.0, jax.random.fold_in(key, 6)
    for position, blocks in pieces:
        heights = jnp.exp(jax.random.uniform(jax.random.fold_in(own, position), (blocks,), jnp.float32, smallest / len(pieces), high / len(pieces)))
        gain = gain * jnp.repeat(heights, dims[position] // blocks).reshape([-1 if axis == position else 1 for axis in range(len(dims))])
    return gain


def assign_block(stream_key, own, number, rows, count, top, most, slope):
    ranking = jax.random.permutation(stream_key, count)
    packed, usual = load_shares(count, rows * top, most, slope, True), load_shares(count, rows * top, most, slope, False)
    places = jnp.arange(count)

    def named(tallies, rotation):
        used = int((tallies > 0).sum())
        fixed = max(1, used // 4)
        moved = fixed + (places - fixed + rotation * (used - fixed)) % max(1, count - fixed)
        return jnp.zeros((count,), jnp.int32).at[ranking[jnp.where(places < fixed, places, moved)]].set(jnp.asarray(tallies, jnp.int32))

    tallies = jnp.where(number % 4 == 0, named(packed, number // 4), named(usual, number - number // 4 - 1))
    mixed = jax.random.permutation(jax.random.fold_in(own, 3), count)
    donor, sink = mixed[0:count // 2 * 2:2], mixed[1:count // 2 * 2:2]
    slack = jnp.minimum(tallies[donor] - 1, most - tallies[sink]) // 2
    slack = jnp.where((donor == ranking[0]) | (sink == ranking[0]) | (tallies[sink] == 0), 0, jnp.maximum(slack, 0))
    moved = jax.random.randint(jax.random.fold_in(own, 4), (count // 2,), 0, 1 << 20) % (slack + 1)
    tallies = tallies.at[donor].add(-moved).at[sink].add(moved)
    labels = jnp.searchsorted(jnp.cumsum(tallies), jnp.arange(rows * top), side="right").astype(jnp.int32)
    table = labels.reshape(top, rows).T
    table = table[jax.random.permutation(jax.random.fold_in(own, 1), rows)]
    rotation = jax.random.randint(jax.random.fold_in(own, 2), (rows, 1), 0, top)
    return jnp.take_along_axis(table, (jnp.arange(top)[None, :] + rotation) % top, axis=1)


def load_shares(number_of, total, bound, lean, full):
    weights = [(1 << 20) // math.isqrt(rank ** lean) + 1 for rank in range(1, number_of + 1)]
    largest = bound if full else min(bound, max(-(-total // number_of), total * weights[0] // sum(weights)))
    least = 1 if total - largest >= number_of - 1 else 0
    given, surplus = [largest] + [least] * (number_of - 1), total - largest - least * (number_of - 1)
    while surplus > 0:
        candidates = [i for i in range(1, number_of) if given[i] < largest] or [i for i in range(1, number_of) if given[i] < bound]
        pool, left = sum([weights[i] for i in candidates]), surplus
        for i in candidates:
            addition = min(bound - given[i], max(1, left * weights[i] // pool), surplus)
            given[i] = given[i] + addition
            surplus = surplus - addition
    return np.array(given)


def gaussian(stream_key, extent, scale, reach, split=(), kind=jnp.bfloat16):
    values = scale * jax.random.normal(stream_key, extent, jnp.float32)
    if split:
        values = values * block_scale(stream_key, extent, split, -0.22, 0.18)
    return jnp.clip(values, -reach, reach).astype(kind)


def heavy_noise(stream_key, extent, scale, bound, split, heavy, kind=jnp.bfloat16):
    values = scale * jax.random.normal(stream_key, extent, jnp.float32)
    if split:
        values = values * block_scale(stream_key, extent, split, -0.22, 0.18)
    return jnp.clip(strengthened(values, jax.random.fold_in(stream_key, 3), *heavy), -bound, bound).astype(kind)


def setup_inputs(seed: int = 0) -> dict:
    streams_of = jax.random.split(jax.random.key(seed), 7)
    tokens = gaussian(streams_of[0], (MICRO, TOKENS, D), 1.0, 6.0, ((1, 4),))
    expert_ids_keys = jax.random.split(jax.random.fold_in(streams_of[1], 1), LAYERS * MICRO * TOKENS // TOK_DEV)
    expert_ids_turns = jax.random.permutation(jax.random.fold_in(streams_of[1], 3), LAYERS * MICRO * TOKENS // TOK_DEV)
    expert_ids = jax.vmap(lambda own, number: assign_block(jax.random.fold_in(streams_of[1], 2), own, number, TOK_DEV, EXPERTS, TOP, CAP, 2))(expert_ids_keys, expert_ids_turns).reshape((LAYERS, MICRO, TOKENS, TOP))
    gates = jnp.clip(jnp.exp(math.log(1.0) - 2.3025851 * jax.random.uniform(streams_of[2], (LAYERS, MICRO, TOKENS, TOP), jnp.float32) ** block_scale(streams_of[2], (LAYERS, MICRO, TOKENS, TOP), ((0, 2), (2, 4)), -0.2, 0.2)), 0.1, 1.0)
    w_gate = gaussian(streams_of[3], (LAYERS, EXPERTS, D, FF), D ** -0.5, 0.109375, ((0, 2), (1, 4), (3, 4)))
    w_up = gaussian(streams_of[4], (LAYERS, EXPERTS, D, FF), D ** -0.5, 0.109375, ((0, 2), (1, 4), (3, 4)))
    w_down = heavy_noise(streams_of[5], (LAYERS, EXPERTS, FF, D), FF ** -0.5, 0.3125, ((0, 2), (1, 4), (2, 4)), (2, 3, 4, 2.0))
    return {"tokens": tokens, "expert_ids": expert_ids, "gates": gates, "w_gate": w_gate, "w_up": w_up, "w_down": w_down}


def pair_slots(route_ids):
    pair_ids = route_ids.reshape(EXPERTS, TOK_DEV * TOP)
    onehot = (pair_ids[:, :, None] == jnp.arange(EXPERTS, dtype=jnp.int32)[None, None, :]).astype(jnp.int32)
    before = jnp.cumsum(onehot, axis=1) - onehot
    slot_ids = lax.optimization_barrier(jnp.sum(before * onehot, axis=2)).astype(jnp.int32)
    return (pair_ids, slot_ids)

def one_layer(layer_in, route_ids, route_gates, gate_weights, up_weights, down_weights):
    pair_ids, slot_ids = pair_slots(route_ids)
    placed = pair_ids * CAP + slot_ids
    blocks = jnp.repeat(layer_in.reshape(EXPERTS, TOK_DEV, D), TOP, axis=1).astype(jnp.float32)
    targets = jnp.arange(CAP, dtype=jnp.int32)

    def one_expert(expert):
        chosen = (placed[:, None, :] == (expert * CAP + targets)[None, :, None]).astype(jnp.float32)
        slot_rows = jnp.einsum('jsp,jpd->jsd', chosen, blocks, precision=lax.Precision.HIGHEST)
        slot_rows = slot_rows.astype(jnp.bfloat16).reshape(EXPERTS * CAP, D)
        squares = lax.optimization_barrier(jnp.mean(jnp.square(slot_rows.astype(jnp.float32)), axis=1, keepdims=True))
        inv_rms = lax.rsqrt(squares + 1e-05)
        gate_act = jnp.dot(slot_rows, gate_weights[expert], preferred_element_type=jnp.float32) * inv_rms
        up_act = jnp.dot(slot_rows, up_weights[expert], preferred_element_type=jnp.float32) * inv_rms
        hidden = (jax.nn.silu(gate_act) * up_act).astype(jnp.bfloat16)
        result = jnp.dot(hidden, down_weights[expert], preferred_element_type=jnp.float32).astype(jnp.bfloat16)
        return result.reshape(EXPERTS, CAP, D)
    outputs = lax.map(one_expert, jnp.arange(EXPERTS, dtype=jnp.int32))
    sources = jnp.arange(EXPERTS, dtype=jnp.int32)[:, None]
    picked = outputs[pair_ids, sources, slot_ids].astype(jnp.float32)
    weights = route_gates.reshape(EXPERTS, TOK_DEV * TOP)
    mixed = (weights[:, :, None] * picked).reshape(EXPERTS, TOK_DEV, TOP, D).sum(axis=2)
    return (layer_in.astype(jnp.float32) + mixed.reshape(TOKENS, D)).astype(jnp.bfloat16)

def reference(tokens, expert_ids, gates, w_gate, w_up, w_down):
    per_layer = [[] for layer in range(LAYERS)]
    for micro_index in range(MICRO):
        current = tokens[micro_index]
        for layer in range(LAYERS):
            current = one_layer(current, expert_ids[layer, micro_index], gates[layer, micro_index], w_gate[layer], w_up[layer], w_down[layer])
            per_layer[layer].append(current)
    return jnp.stack([jnp.stack(stack_list, axis=0) for stack_list in per_layer], axis=0)
```

```python
import jax
import jax.numpy as jnp
from jax import lax
from jax.sharding import PartitionSpec as P

TOP = 2
CAP = 16
AXES = ("dp", "pipe", "expert")
SMALL_GROUP = 8


class Ring:
    def __init__(self, n):
        self.n = n
        self.xor = n & (n - 1) == 0

    def ahead(self, me, s):
        return me ^ s if self.xor else (me + s) % self.n

    def behind(self, me, s):
        return me ^ s if self.xor else (me - s) % self.n

    def place(self, target, me):
        return target ^ me if self.xor else (target - me) % self.n


def build_maps(route_ids, route_gates, ring, me, rows_all):
    experts = ring.n
    flat_ids = route_ids.reshape(-1)
    onehot = (flat_ids[:, None] == jnp.arange(experts, dtype=jnp.int32)[None, :]).astype(jnp.int32)
    before = jnp.cumsum(onehot, axis=0) - onehot
    slot = jnp.sum(before * onehot, axis=1)
    placed = ring.place(flat_ids, me) * CAP + slot
    matches = jnp.arange(rows_all, dtype=jnp.int32)[:, None] == placed[None, :]
    dispatch_map = jnp.sum(matches.astype(jnp.float32).reshape(rows_all, -1, TOP), axis=2).astype(jnp.bfloat16)
    combine_map = jnp.sum(
        jnp.where(matches, route_gates.reshape(-1)[None, :], 0.0).reshape(rows_all, -1, TOP), axis=2
    )
    return dispatch_map, combine_map


def per_device(tokens, expert_ids, gates, w_gate, w_up, w_down):
    n_dp = lax.axis_size("dp")
    n_pipe = lax.axis_size("pipe")
    n_exp = lax.axis_size("expert")
    micro, tok_rows, width = tokens.shape
    units = w_gate.shape[3]
    columns = width // n_dp
    rows_all = n_exp * CAP
    d_me = lax.axis_index("dp")
    p_me = lax.axis_index("pipe")
    e_me = lax.axis_index("expert")
    dring = Ring(n_dp)
    ering = Ring(n_exp)
    small_dp = n_dp <= SMALL_GROUP

    def lin(d, p, e):
        return (d * n_pipe + p) * n_exp + e

    def expert_pairs(p, s, back):
        step = ering.behind if back else ering.ahead
        return [(lin(d, p, e), lin(d, p, step(e, s))) for d in range(n_dp) for e in range(n_exp)]

    def dp_pairs(p, s):
        return [(lin(d, p, e), lin(dring.ahead(d, s), p, e)) for d in range(n_dp) for e in range(n_exp)]

    gate_local = w_gate[0, 0]
    up_local = w_up[0, 0]
    down_local = w_down[0, 0]

    if small_dp:
        down_parts = []
        for s in range(n_dp):
            piece = lax.dynamic_slice_in_dim(down_local, dring.ahead(d_me, s) * columns, columns, 1)
            if s:
                piece = lax.ppermute(piece, "dp", [(i, dring.ahead(i, s)) for i in range(n_dp)])
            down_parts.append(piece)
        down_full = jnp.concatenate(down_parts, axis=0)
    else:
        down_full = lax.all_to_all(down_local, "dp", 1, 0, tiled=True)

    route_ids = expert_ids[0]
    route_gates = gates[0]
    maps = [build_maps(route_ids[m], route_gates[m], ering, e_me, rows_all) for m in range(micro)]
    dispatch_map = jnp.stack([mp[0] for mp in maps])
    combine_map = jnp.stack([mp[1] for mp in maps])

    def layer(current, p):
        outgoing = jnp.einsum("mrt,mtd->mrd", dispatch_map, current, preferred_element_type=jnp.float32)
        outgoing = outgoing.astype(jnp.bfloat16).reshape(micro, n_exp, CAP, width)
        arrived = [outgoing[:, 0]]
        for s in range(1, n_exp):
            arrived.append(lax.ppermute(outgoing[:, s], AXES, expert_pairs(p, s, False)))
        flat_rows = jnp.stack(arrived, axis=1).reshape(-1, width)
        squares = jnp.mean(jnp.square(flat_rows.astype(jnp.float32)), axis=1, keepdims=True)
        inv_rms = lax.rsqrt(squares + 1e-05)
        gate_act = jnp.dot(flat_rows, gate_local, preferred_element_type=jnp.float32) * inv_rms
        up_act = jnp.dot(flat_rows, up_local, preferred_element_type=jnp.float32) * inv_rms
        hidden = (jax.nn.silu(gate_act) * up_act).astype(jnp.bfloat16)
        if small_dp:
            parts = [hidden]
            for s in range(1, n_dp):
                parts.append(lax.ppermute(hidden, AXES, dp_pairs(p, s)))
            hidden_full = jnp.concatenate(parts, axis=1)
        else:
            hidden_full = lax.all_gather(hidden, "dp", axis=1, tiled=True)
        expert_out = jnp.dot(hidden_full, down_full, preferred_element_type=jnp.float32).astype(jnp.bfloat16)
        expert_out = expert_out.reshape(micro, n_exp, CAP, columns)
        returned = [expert_out[:, 0]]
        for s in range(1, n_exp):
            returned.append(lax.ppermute(expert_out[:, s], AXES, expert_pairs(p, s, True)))
        returned = jnp.stack(returned, axis=1).reshape(micro, rows_all, columns)
        mixed = jnp.einsum(
            "mrt,mrc->mtc",
            combine_map,
            returned.astype(jnp.float32),
            precision=lax.Precision.HIGHEST,
            preferred_element_type=jnp.float32,
        )
        current_cols = lax.dynamic_slice_in_dim(current, d_me * columns, columns, 2)
        return (current_cols.astype(jnp.float32) + mixed).astype(jnp.bfloat16)

    current = tokens
    result = None
    for p in range(n_pipe):
        cols = layer(current, p)
        result = cols if result is None else jnp.where(p_me == p, cols, result)
        if p + 1 < n_pipe:
            if small_dp:
                parts = []
                for s in range(n_dp):
                    pairs = [
                        (lin(d, p, e), lin(dring.ahead(d, s), p + 1, e)) for d in range(n_dp) for e in range(n_exp)
                    ]
                    parts.append(lax.ppermute(cols, AXES, pairs))
                stacked = jnp.stack(parts)
                order = jnp.stack([dring.place(d_me, k) for k in range(n_dp)])
                stacked = jnp.take(stacked, order, axis=0)
                current = jnp.transpose(stacked, (1, 2, 0, 3)).reshape(micro, tok_rows, width)
            else:
                full = lax.all_gather(cols, "dp", axis=2, tiled=True)
                current = lax.ppermute(full, "pipe", [(p, p + 1)])
    return result[None]


def solution(mesh):
    return jax.shard_map(
        per_device,
        mesh=mesh,
        in_specs=(
            P(None, "expert", None),
            P("pipe", None, "expert", None),
            P("pipe", None, "expert", None),
            P("pipe", "expert", None, "dp"),
            P("pipe", "expert", None, "dp"),
            P("pipe", "expert", "dp", None),
        ),
        out_specs=P("pipe", None, "expert", "dp"),
        check_vma=False,
    )
```

```python
import jax
import jax.numpy as jnp
from jax import lax
from jax.sharding import PartitionSpec as P

TOP = 2
CAP = 16
AXES = ("dp", "pipe", "expert")
SMALL_GROUP = 8


class Ring:
    def __init__(self, n):
        self.n = n
        self.xor = n & (n - 1) == 0

    def ahead(self, me, s):
        return me ^ s if self.xor else (me + s) % self.n

    def behind(self, me, s):
        return me ^ s if self.xor else (me - s) % self.n

    def place(self, target, me):
        return target ^ me if self.xor else (target - me) % self.n


def build_maps(route_ids, route_gates, ring, me, rows_all):
    experts = ring.n
    flat_ids = route_ids.reshape(-1)
    onehot = (flat_ids[:, None] == jnp.arange(experts, dtype=jnp.int32)[None, :]).astype(jnp.int32)
    before = jnp.cumsum(onehot, axis=0) - onehot
    slot = jnp.sum(before * onehot, axis=1)
    placed = ring.place(flat_ids, me) * CAP + slot
    matches = jnp.arange(rows_all, dtype=jnp.int32)[:, None] == placed[None, :]
    dispatch_map = jnp.sum(matches.astype(jnp.float32).reshape(rows_all, -1, TOP), axis=2).astype(jnp.bfloat16)
    combine_map = jnp.sum(
        jnp.where(matches, route_gates.reshape(-1)[None, :], 0.0).reshape(rows_all, -1, TOP), axis=2
    )
    return dispatch_map, combine_map


def per_device(tokens, expert_ids, gates, w_gate, w_up, w_down):
    n_dp = lax.axis_size("dp")
    n_pipe = lax.axis_size("pipe")
    n_exp = lax.axis_size("expert")
    micro, tok_rows, width = tokens.shape
    units = w_gate.shape[3]
    columns = width // n_dp
    rows_all = n_exp * CAP
    d_me = lax.axis_index("dp")
    p_me = lax.axis_index("pipe")
    e_me = lax.axis_index("expert")
    dring = Ring(n_dp)
    ering = Ring(n_exp)
    small_dp = n_dp <= SMALL_GROUP

    def lin(d, p, e):
        return (d * n_pipe + p) * n_exp + e

    def expert_pairs(p, s, back):
        step = ering.behind if back else ering.ahead
        return [(lin(d, p, e), lin(d, p, step(e, s))) for d in range(n_dp) for e in range(n_exp)]

    def dp_pairs(p, s):
        return [(lin(d, p, e), lin(dring.ahead(d, s), p, e)) for d in range(n_dp) for e in range(n_exp)]

    gate_local = w_gate[0, 0]
    up_local = w_up[0, 0]
    down_local = w_down[0, 0]

    def resplit_down(p, anchor):
        if not small_dp:
            return lax.all_to_all(down_local, "dp", 1, 0, tiled=True), anchor
        parts = []
        for s in range(n_dp):
            piece = lax.dynamic_slice_in_dim(down_local, dring.ahead(d_me, s) * columns, columns, 1)
            if s:
                if anchor is not None:
                    piece, anchor = lax.optimization_barrier((piece, anchor))
                piece = lax.ppermute(piece, AXES, dp_pairs(p, s))
            parts.append(piece)
        return jnp.concatenate(parts, axis=0), anchor

    route_ids = expert_ids[0]
    route_gates = gates[0]
    maps = [build_maps(route_ids[m], route_gates[m], ering, e_me, rows_all) for m in range(micro)]
    dispatch_map = jnp.stack([mp[0] for mp in maps])
    combine_map = jnp.stack([mp[1] for mp in maps])

    def layer(current, p, down_full):
        outgoing = jnp.einsum("mrt,mtd->mrd", dispatch_map, current, preferred_element_type=jnp.float32)
        outgoing = outgoing.astype(jnp.bfloat16).reshape(micro, n_exp, CAP, width)
        arrived = [outgoing[:, 0]]
        for s in range(1, n_exp):
            arrived.append(lax.ppermute(outgoing[:, s], AXES, expert_pairs(p, s, False)))
        flat_rows = jnp.stack(arrived, axis=1).reshape(-1, width)
        squares = jnp.mean(jnp.square(flat_rows.astype(jnp.float32)), axis=1, keepdims=True)
        inv_rms = lax.rsqrt(squares + 1e-05)
        gate_act = jnp.dot(flat_rows, gate_local, preferred_element_type=jnp.float32) * inv_rms
        up_act = jnp.dot(flat_rows, up_local, preferred_element_type=jnp.float32) * inv_rms
        hidden = (jax.nn.silu(gate_act) * up_act).astype(jnp.bfloat16)
        if small_dp:
            parts = [hidden]
            for s in range(1, n_dp):
                parts.append(lax.ppermute(hidden, AXES, dp_pairs(p, s)))
            hidden_full = jnp.concatenate(parts, axis=1)
        else:
            hidden_full = lax.all_gather(hidden, "dp", axis=1, tiled=True)
        expert_out = jnp.dot(hidden_full, down_full, preferred_element_type=jnp.float32).astype(jnp.bfloat16)
        expert_out = expert_out.reshape(micro, n_exp, CAP, columns)
        returned = [expert_out[:, 0]]
        for s in range(1, n_exp):
            returned.append(lax.ppermute(expert_out[:, s], AXES, expert_pairs(p, s, True)))
        returned = jnp.stack(returned, axis=1).reshape(micro, rows_all, columns)
        mixed = jnp.einsum(
            "mrt,mrc->mtc",
            combine_map,
            returned.astype(jnp.float32),
            precision=lax.Precision.HIGHEST,
            preferred_element_type=jnp.float32,
        )
        current_cols = lax.dynamic_slice_in_dim(current, d_me * columns, columns, 2)
        return (current_cols.astype(jnp.float32) + mixed).astype(jnp.bfloat16)

    current = tokens
    result = None
    for p in range(n_pipe):
        down_full, anchor = resplit_down(p, current if p else None)
        current = current if anchor is None else anchor
        cols = layer(current, p, down_full)
        result = cols if result is None else jnp.where(p_me == p, cols, result)
        if p + 1 < n_pipe:
            if small_dp:
                parts = []
                for s in range(n_dp):
                    pairs = [
                        (lin(d, p, e), lin(dring.ahead(d, s), p + 1, e)) for d in range(n_dp) for e in range(n_exp)
                    ]
                    parts.append(lax.ppermute(cols, AXES, pairs))
                stacked = jnp.stack(parts)
                order = jnp.stack([dring.place(d_me, k) for k in range(n_dp)])
                stacked = jnp.take(stacked, order, axis=0)
                current = jnp.transpose(stacked, (1, 2, 0, 3)).reshape(micro, tok_rows, width)
            else:
                full = lax.all_gather(cols, "dp", axis=2, tiled=True)
                current = lax.ppermute(full, "pipe", [(p, p + 1)])
    return result[None]


def solution(mesh):
    return jax.shard_map(
        per_device,
        mesh=mesh,
        in_specs=(
            P(None, "expert", None),
            P("pipe", None, "expert", None),
            P("pipe", None, "expert", None),
            P("pipe", "expert", None, "dp"),
            P("pipe", "expert", None, "dp"),
            P("pipe", "expert", "dp", None),
        ),
        out_specs=P("pipe", None, "expert", "dp"),
        check_vma=False,
    )
```

```python
import jax
import jax.numpy as jnp
from jax import lax
from jax.sharding import PartitionSpec as P

TOP = 2
CAP = 16
AXES = ("dp", "pipe", "expert")
SMALL_GROUP = 8


class Ring:
    def __init__(self, n):
        self.n = n
        self.xor = n & (n - 1) == 0

    def ahead(self, me, s):
        return me ^ s if self.xor else (me + s) % self.n

    def behind(self, me, s):
        return me ^ s if self.xor else (me - s) % self.n

    def place(self, target, me):
        return target ^ me if self.xor else (target - me) % self.n


def build_maps(route_ids, route_gates, ring, me, rows_all):
    experts = ring.n
    flat_ids = route_ids.reshape(-1)
    onehot = (flat_ids[:, None] == jnp.arange(experts, dtype=jnp.int32)[None, :]).astype(jnp.int32)
    before = jnp.cumsum(onehot, axis=0) - onehot
    slot = jnp.sum(before * onehot, axis=1)
    placed = ring.place(flat_ids, me) * CAP + slot
    matches = jnp.arange(rows_all, dtype=jnp.int32)[:, None] == placed[None, :]
    dispatch_map = jnp.sum(matches.astype(jnp.float32).reshape(rows_all, -1, TOP), axis=2).astype(jnp.bfloat16)
    combine_map = jnp.sum(
        jnp.where(matches, route_gates.reshape(-1)[None, :], 0.0).reshape(rows_all, -1, TOP), axis=2
    )
    return dispatch_map, combine_map


def per_device(tokens, expert_ids, gates, w_gate, w_up, w_down):
    n_dp = lax.axis_size("dp")
    n_pipe = lax.axis_size("pipe")
    n_exp = lax.axis_size("expert")
    micro, tok_rows, width = tokens.shape
    units = w_gate.shape[3]
    columns = width // n_dp
    rows_all = n_exp * CAP
    d_me = lax.axis_index("dp")
    p_me = lax.axis_index("pipe")
    e_me = lax.axis_index("expert")
    dring = Ring(n_dp)
    ering = Ring(n_exp)
    small_dp = n_dp <= SMALL_GROUP

    def lin(d, p, e):
        return (d * n_pipe + p) * n_exp + e

    def expert_pairs(p, s, back):
        step = ering.behind if back else ering.ahead
        return [(lin(d, p, e), lin(d, p, step(e, s))) for d in range(n_dp) for e in range(n_exp)]

    def dp_pairs(p, s):
        return [(lin(d, p, e), lin(dring.ahead(d, s), p, e)) for d in range(n_dp) for e in range(n_exp)]

    gate_local = w_gate[0, 0]
    up_local = w_up[0, 0]
    down_local = w_down[0, 0]

    route_ids = expert_ids[0]
    route_gates = gates[0]
    maps = [build_maps(route_ids[m], route_gates[m], ering, e_me, rows_all) for m in range(micro)]
    dispatch_map = jnp.stack([mp[0] for mp in maps])
    combine_map = jnp.stack([mp[1] for mp in maps])

    def layer(current, p):
        outgoing = jnp.einsum("mrt,mtd->mrd", dispatch_map, current, preferred_element_type=jnp.float32)
        outgoing = outgoing.astype(jnp.bfloat16).reshape(micro, n_exp, CAP, width)
        arrived = [outgoing[:, 0]]
        for s in range(1, n_exp):
            arrived.append(lax.ppermute(outgoing[:, s], AXES, expert_pairs(p, s, False)))
        flat_rows = jnp.stack(arrived, axis=1).reshape(-1, width)
        squares = jnp.mean(jnp.square(flat_rows.astype(jnp.float32)), axis=1, keepdims=True)
        inv_rms = lax.rsqrt(squares + 1e-05)
        gate_act = jnp.dot(flat_rows, gate_local, preferred_element_type=jnp.float32) * inv_rms
        up_act = jnp.dot(flat_rows, up_local, preferred_element_type=jnp.float32) * inv_rms
        hidden = (jax.nn.silu(gate_act) * up_act).astype(jnp.bfloat16)
        if small_dp:
            hidden_t = hidden.T
            hidden_parts = [hidden_t]
            down_parts = [lax.dynamic_slice_in_dim(down_local, d_me * columns, columns, 1)]
            for s in range(1, n_dp):
                piece = lax.dynamic_slice_in_dim(down_local, dring.ahead(d_me, s) * columns, columns, 1)
                packet = lax.ppermute(jnp.concatenate([hidden_t, piece], axis=1), AXES, dp_pairs(p, s))
                hidden_parts.append(packet[:, : hidden_t.shape[1]])
                down_parts.append(packet[:, hidden_t.shape[1] :])
            expert_out = lax.dot_general(
                jnp.concatenate(hidden_parts, axis=0),
                jnp.concatenate(down_parts, axis=0),
                (((0,), (0,)), ((), ())),
                preferred_element_type=jnp.float32,
            ).astype(jnp.bfloat16)
        else:
            hidden_full = lax.all_gather(hidden, "dp", axis=1, tiled=True)
            down_full = lax.all_to_all(down_local, "dp", 1, 0, tiled=True)
            expert_out = jnp.dot(hidden_full, down_full, preferred_element_type=jnp.float32).astype(jnp.bfloat16)
        expert_out = expert_out.reshape(micro, n_exp, CAP, columns)
        returned = [expert_out[:, 0]]
        for s in range(1, n_exp):
            returned.append(lax.ppermute(expert_out[:, s], AXES, expert_pairs(p, s, True)))
        returned = jnp.stack(returned, axis=1).reshape(micro, rows_all, columns)
        mixed = jnp.einsum(
            "mrt,mrc->mtc",
            combine_map,
            returned.astype(jnp.float32),
            precision=lax.Precision.HIGHEST,
            preferred_element_type=jnp.float32,
        )
        current_cols = lax.dynamic_slice_in_dim(current, d_me * columns, columns, 2)
        return (current_cols.astype(jnp.float32) + mixed).astype(jnp.bfloat16)

    current = tokens
    result = None
    for p in range(n_pipe):
        cols = layer(current, p)
        result = cols if result is None else jnp.where(p_me == p, cols, result)
        if p + 1 < n_pipe:
            if small_dp:
                parts = []
                for s in range(n_dp):
                    pairs = [
                        (lin(d, p, e), lin(dring.ahead(d, s), p + 1, e)) for d in range(n_dp) for e in range(n_exp)
                    ]
                    parts.append(lax.ppermute(cols, AXES, pairs))
                stacked = jnp.stack(parts)
                order = jnp.stack([dring.place(d_me, k) for k in range(n_dp)])
                stacked = jnp.take(stacked, order, axis=0)
                current = jnp.transpose(stacked, (1, 2, 0, 3)).reshape(micro, tok_rows, width)
            else:
                full = lax.all_gather(cols, "dp", axis=2, tiled=True)
                current = lax.ppermute(full, "pipe", [(p, p + 1)])
    return result[None]


def solution(mesh):
    return jax.shard_map(
        per_device,
        mesh=mesh,
        in_specs=(
            P(None, "expert", None),
            P("pipe", None, "expert", None),
            P("pipe", None, "expert", None),
            P("pipe", "expert", None, "dp"),
            P("pipe", "expert", None, "dp"),
            P("pipe", "expert", "dp", None),
        ),
        out_specs=P("pipe", None, "expert", "dp"),
        check_vma=False,
    )
```

```python
import jax
import jax.numpy as jnp
from jax import lax
from jax.sharding import PartitionSpec as P

TOP = 2
CAP = 16
AXES = ("dp", "pipe", "expert")
SMALL_GROUP = 8


class Ring:
    def __init__(self, n):
        self.n = n
        self.xor = n & (n - 1) == 0

    def ahead(self, me, s):
        return me ^ s if self.xor else (me + s) % self.n

    def behind(self, me, s):
        return me ^ s if self.xor else (me - s) % self.n

    def place(self, target, me):
        return target ^ me if self.xor else (target - me) % self.n


def build_maps(route_ids, route_gates, ring, me, rows_all):
    experts = ring.n
    flat_ids = route_ids.reshape(-1)
    onehot = (flat_ids[:, None] == jnp.arange(experts, dtype=jnp.int32)[None, :]).astype(jnp.int32)
    before = jnp.cumsum(onehot, axis=0) - onehot
    slot = jnp.sum(before * onehot, axis=1)
    placed = ring.place(flat_ids, me) * CAP + slot
    matches = jnp.arange(rows_all, dtype=jnp.int32)[:, None] == placed[None, :]
    dispatch_map = jnp.sum(matches.astype(jnp.float32).reshape(rows_all, -1, TOP), axis=2).astype(jnp.bfloat16)
    combine_map = jnp.sum(
        jnp.where(matches, route_gates.reshape(-1)[None, :], 0.0).reshape(rows_all, -1, TOP), axis=2
    )
    return dispatch_map, combine_map


def per_device(tokens, expert_ids, gates, w_gate, w_up, w_down):
    n_dp = lax.axis_size("dp")
    n_pipe = lax.axis_size("pipe")
    n_exp = lax.axis_size("expert")
    micro, tok_rows, width = tokens.shape
    units = w_gate.shape[3]
    columns = width // n_dp
    rows_all = n_exp * CAP
    d_me = lax.axis_index("dp")
    p_me = lax.axis_index("pipe")
    e_me = lax.axis_index("expert")
    dring = Ring(n_dp)
    ering = Ring(n_exp)
    small_dp = n_dp <= SMALL_GROUP

    def lin(d, p, e):
        return (d * n_pipe + p) * n_exp + e

    def expert_pairs(p, s, back):
        step = ering.behind if back else ering.ahead
        return [(lin(d, p, e), lin(d, p, step(e, s))) for d in range(n_dp) for e in range(n_exp)]

    def dp_pairs(p, s):
        return [(lin(d, p, e), lin(dring.ahead(d, s), p, e)) for d in range(n_dp) for e in range(n_exp)]

    gate_local = w_gate[0, 0]
    up_local = w_up[0, 0]
    down_local = w_down[0, 0]

    down_full = {}
    for p in range(1, n_pipe):
        if small_dp:
            parts = [lax.dynamic_slice_in_dim(down_local, d_me * columns, columns, 1)]
            for s in range(1, n_dp):
                piece = lax.dynamic_slice_in_dim(down_local, dring.ahead(d_me, s) * columns, columns, 1)
                parts.append(lax.ppermute(piece, AXES, dp_pairs(p, s)))
            down_full[p] = jnp.concatenate(parts, axis=0)
        else:
            down_full[p] = lax.all_to_all(down_local, "dp", 1, 0, tiled=True)

    route_ids = expert_ids[0]
    route_gates = gates[0]
    maps = [build_maps(route_ids[m], route_gates[m], ering, e_me, rows_all) for m in range(micro)]
    dispatch_map = jnp.stack([mp[0] for mp in maps])
    combine_map = jnp.stack([mp[1] for mp in maps])

    def layer(current, p):
        outgoing = jnp.einsum("mrt,mtd->mrd", dispatch_map, current, preferred_element_type=jnp.float32)
        outgoing = outgoing.astype(jnp.bfloat16).reshape(micro, n_exp, CAP, width)
        arrived = [outgoing[:, 0]]
        for s in range(1, n_exp):
            arrived.append(lax.ppermute(outgoing[:, s], AXES, expert_pairs(p, s, False)))
        flat_rows = jnp.stack(arrived, axis=1).reshape(-1, width)
        squares = jnp.mean(jnp.square(flat_rows.astype(jnp.float32)), axis=1, keepdims=True)
        inv_rms = lax.rsqrt(squares + 1e-05)
        gate_act = jnp.dot(flat_rows, gate_local, preferred_element_type=jnp.float32) * inv_rms
        up_act = jnp.dot(flat_rows, up_local, preferred_element_type=jnp.float32) * inv_rms
        hidden = (jax.nn.silu(gate_act) * up_act).astype(jnp.bfloat16)
        if p == 0 and small_dp:
            partial = jnp.dot(hidden, down_local, preferred_element_type=jnp.float32)
            total = lax.dynamic_slice_in_dim(partial, d_me * columns, columns, 1)
            for s in range(1, n_dp):
                chunk = lax.dynamic_slice_in_dim(partial, dring.ahead(d_me, s) * columns, columns, 1)
                total = total + lax.ppermute(chunk.astype(jnp.bfloat16), AXES, dp_pairs(p, s)).astype(jnp.float32)
            expert_out = total.astype(jnp.bfloat16)
        else:
            if p == 0:
                down_p = lax.all_to_all(down_local, "dp", 1, 0, tiled=True)
            else:
                down_p = down_full[p]
            if small_dp:
                parts = [hidden]
                for s in range(1, n_dp):
                    parts.append(lax.ppermute(hidden, AXES, dp_pairs(p, s)))
                hidden_full = jnp.concatenate(parts, axis=1)
            else:
                hidden_full = lax.all_gather(hidden, "dp", axis=1, tiled=True)
            expert_out = jnp.dot(hidden_full, down_p, preferred_element_type=jnp.float32).astype(jnp.bfloat16)
        expert_out = expert_out.reshape(micro, n_exp, CAP, columns)
        returned = [expert_out[:, 0]]
        for s in range(1, n_exp):
            returned.append(lax.ppermute(expert_out[:, s], AXES, expert_pairs(p, s, True)))
        returned = jnp.stack(returned, axis=1).reshape(micro, rows_all, columns)
        mixed = jnp.einsum(
            "mrt,mrc->mtc",
            combine_map,
            returned.astype(jnp.float32),
            precision=lax.Precision.HIGHEST,
            preferred_element_type=jnp.float32,
        )
        current_cols = lax.dynamic_slice_in_dim(current, d_me * columns, columns, 2)
        return (current_cols.astype(jnp.float32) + mixed).astype(jnp.bfloat16)

    current = tokens
    if down_full:
        down_full, current = lax.optimization_barrier((down_full, current))
    result = None
    for p in range(n_pipe):
        cols = layer(current, p)
        result = cols if result is None else jnp.where(p_me == p, cols, result)
        if p + 1 < n_pipe:
            if small_dp:
                parts = []
                for s in range(n_dp):
                    pairs = [
                        (lin(d, p, e), lin(dring.ahead(d, s), p + 1, e)) for d in range(n_dp) for e in range(n_exp)
                    ]
                    parts.append(lax.ppermute(cols, AXES, pairs))
                stacked = jnp.stack(parts)
                order = jnp.stack([dring.place(d_me, k) for k in range(n_dp)])
                stacked = jnp.take(stacked, order, axis=0)
                current = jnp.transpose(stacked, (1, 2, 0, 3)).reshape(micro, tok_rows, width)
            else:
                full = lax.all_gather(cols, "dp", axis=2, tiled=True)
                current = lax.ppermute(full, "pipe", [(p, p + 1)])
    return result[None]


def solution(mesh):
    return jax.shard_map(
        per_device,
        mesh=mesh,
        in_specs=(
            P(None, "expert", None),
            P("pipe", None, "expert", None),
            P("pipe", None, "expert", None),
            P("pipe", "expert", None, "dp"),
            P("pipe", "expert", None, "dp"),
            P("pipe", "expert", "dp", None),
        ),
        out_specs=P("pipe", None, "expert", "dp"),
        check_vma=False,
    )
```

```python
import jax
import jax.numpy as jnp
from jax import lax
from jax.sharding import PartitionSpec as P

TOP = 2
CAP = 16
AXES = ("dp", "pipe", "expert")
SMALL_GROUP = 8


class Ring:
    def __init__(self, n):
        self.n = n
        self.xor = n & (n - 1) == 0

    def ahead(self, me, s):
        return me ^ s if self.xor else (me + s) % self.n

    def behind(self, me, s):
        return me ^ s if self.xor else (me - s) % self.n

    def place(self, target, me):
        return target ^ me if self.xor else (target - me) % self.n


def hyper_all_to_all(chunks, pairs_for):
    held = [(k, 0, chunk) for k, chunk in enumerate(chunks)]
    bit = 1
    while bit < len(chunks):
        send = [h for h in held if h[0] & bit]
        keep = [h for h in held if not h[0] & bit]
        got = lax.ppermute(jnp.stack([h[2] for h in send]), AXES, pairs_for(bit))
        held = keep + [(k ^ bit, j ^ bit, got[i]) for i, (k, j, _) in enumerate(send)]
        bit *= 2
    arrived = [None] * len(chunks)
    for k, j, chunk in held:
        arrived[j] = chunk
    return arrived


def hyper_all_gather(value, n, pairs_for):
    held = [(0, value)]
    bit = 1
    while bit < n:
        got = lax.ppermute(jnp.stack([h[1] for h in held]), AXES, pairs_for(bit))
        held = held + [(j ^ bit, got[i]) for i, (j, _) in enumerate(held)]
        bit *= 2
    arrived = [None] * n
    for j, chunk in held:
        arrived[j] = chunk
    return arrived


def build_maps(route_ids, route_gates, ring, me, rows_all):
    experts = ring.n
    flat_ids = route_ids.reshape(-1)
    onehot = (flat_ids[:, None] == jnp.arange(experts, dtype=jnp.int32)[None, :]).astype(jnp.int32)
    before = jnp.cumsum(onehot, axis=0) - onehot
    slot = jnp.sum(before * onehot, axis=1)
    placed = ring.place(flat_ids, me) * CAP + slot
    matches = jnp.arange(rows_all, dtype=jnp.int32)[:, None] == placed[None, :]
    dispatch_map = jnp.sum(matches.astype(jnp.float32).reshape(rows_all, -1, TOP), axis=2).astype(jnp.bfloat16)
    combine_map = jnp.sum(
        jnp.where(matches, route_gates.reshape(-1)[None, :], 0.0).reshape(rows_all, -1, TOP), axis=2
    )
    return dispatch_map, combine_map


def per_device(tokens, expert_ids, gates, w_gate, w_up, w_down):
    n_dp = lax.axis_size("dp")
    n_pipe = lax.axis_size("pipe")
    n_exp = lax.axis_size("expert")
    micro, tok_rows, width = tokens.shape
    units = w_gate.shape[3]
    columns = width // n_dp
    rows_all = n_exp * CAP
    d_me = lax.axis_index("dp")
    p_me = lax.axis_index("pipe")
    e_me = lax.axis_index("expert")
    dring = Ring(n_dp)
    ering = Ring(n_exp)
    small_dp = n_dp <= SMALL_GROUP

    def lin(d, p, e):
        return (d * n_pipe + p) * n_exp + e

    def expert_pairs(p, s, back):
        step = ering.behind if back else ering.ahead
        return [(lin(d, p, e), lin(d, p, step(e, s))) for d in range(n_dp) for e in range(n_exp)]

    def dp_pairs(p, s):
        return [(lin(d, p, e), lin(dring.ahead(d, s), p, e)) for d in range(n_dp) for e in range(n_exp)]

    def dp_all(bit):
        return [(lin(d, p, e), lin(d ^ bit, p, e)) for d in range(n_dp) for p in range(n_pipe) for e in range(n_exp)]

    gate_local = w_gate[0, 0]
    up_local = w_up[0, 0]
    down_local = w_down[0, 0]

    if small_dp and dring.xor:
        chunks = [lax.dynamic_slice_in_dim(down_local, (d_me ^ k) * columns, columns, 1) for k in range(n_dp)]
        down_full = jnp.concatenate(
            hyper_all_to_all(chunks, dp_all), axis=0
        )
    elif small_dp:
        down_parts = []
        for s in range(n_dp):
            piece = lax.dynamic_slice_in_dim(down_local, dring.ahead(d_me, s) * columns, columns, 1)
            if s:
                piece = lax.ppermute(piece, "dp", [(i, dring.ahead(i, s)) for i in range(n_dp)])
            down_parts.append(piece)
        down_full = jnp.concatenate(down_parts, axis=0)
    else:
        down_full = lax.all_to_all(down_local, "dp", 1, 0, tiled=True)

    route_ids = expert_ids[0]
    route_gates = gates[0]
    maps = [build_maps(route_ids[m], route_gates[m], ering, e_me, rows_all) for m in range(micro)]
    dispatch_map = jnp.stack([mp[0] for mp in maps])
    combine_map = jnp.stack([mp[1] for mp in maps])

    def layer(current, p):
        outgoing = jnp.einsum("mrt,mtd->mrd", dispatch_map, current, preferred_element_type=jnp.float32)
        outgoing = outgoing.astype(jnp.bfloat16).reshape(micro, n_exp, CAP, width)
        if ering.xor:
            arrived = hyper_all_to_all([outgoing[:, s] for s in range(n_exp)], lambda bit: expert_pairs(p, bit, False))
        else:
            arrived = [outgoing[:, 0]]
            for s in range(1, n_exp):
                arrived.append(lax.ppermute(outgoing[:, s], AXES, expert_pairs(p, s, False)))
        flat_rows = jnp.stack(arrived, axis=1).reshape(-1, width)
        squares = jnp.mean(jnp.square(flat_rows.astype(jnp.float32)), axis=1, keepdims=True)
        inv_rms = lax.rsqrt(squares + 1e-05)
        gate_act = jnp.dot(flat_rows, gate_local, preferred_element_type=jnp.float32) * inv_rms
        up_act = jnp.dot(flat_rows, up_local, preferred_element_type=jnp.float32) * inv_rms
        hidden = (jax.nn.silu(gate_act) * up_act).astype(jnp.bfloat16)
        if small_dp and dring.xor:
            hidden_full = jnp.concatenate(hyper_all_gather(hidden, n_dp, lambda bit: dp_pairs(p, bit)), axis=1)
        elif small_dp:
            parts = [hidden]
            for s in range(1, n_dp):
                parts.append(lax.ppermute(hidden, AXES, dp_pairs(p, s)))
            hidden_full = jnp.concatenate(parts, axis=1)
        else:
            hidden_full = lax.all_gather(hidden, "dp", axis=1, tiled=True)
        expert_out = jnp.dot(hidden_full, down_full, preferred_element_type=jnp.float32).astype(jnp.bfloat16)
        expert_out = expert_out.reshape(micro, n_exp, CAP, columns)
        if ering.xor:
            returned = hyper_all_to_all([expert_out[:, s] for s in range(n_exp)], lambda bit: expert_pairs(p, bit, True))
        else:
            returned = [expert_out[:, 0]]
            for s in range(1, n_exp):
                returned.append(lax.ppermute(expert_out[:, s], AXES, expert_pairs(p, s, True)))
        returned = jnp.stack(returned, axis=1).reshape(micro, rows_all, columns)
        mixed = jnp.einsum(
            "mrt,mrc->mtc",
            combine_map,
            returned.astype(jnp.float32),
            precision=lax.Precision.HIGHEST,
            preferred_element_type=jnp.float32,
        )
        current_cols = lax.dynamic_slice_in_dim(current, d_me * columns, columns, 2)
        return (current_cols.astype(jnp.float32) + mixed).astype(jnp.bfloat16)

    current = tokens
    result = None
    for p in range(n_pipe):
        cols = layer(current, p)
        result = cols if result is None else jnp.where(p_me == p, cols, result)
        if p + 1 < n_pipe:
            if small_dp:
                parts = []
                for s in range(n_dp):
                    pairs = [
                        (lin(d, p, e), lin(dring.ahead(d, s), p + 1, e)) for d in range(n_dp) for e in range(n_exp)
                    ]
                    parts.append(lax.ppermute(cols, AXES, pairs))
                stacked = jnp.stack(parts)
                order = jnp.stack([dring.place(d_me, k) for k in range(n_dp)])
                stacked = jnp.take(stacked, order, axis=0)
                current = jnp.transpose(stacked, (1, 2, 0, 3)).reshape(micro, tok_rows, width)
            else:
                full = lax.all_gather(cols, "dp", axis=2, tiled=True)
                current = lax.ppermute(full, "pipe", [(p, p + 1)])
    return result[None]


def solution(mesh):
    return jax.shard_map(
        per_device,
        mesh=mesh,
        in_specs=(
            P(None, "expert", None),
            P("pipe", None, "expert", None),
            P("pipe", None, "expert", None),
            P("pipe", "expert", None, "dp"),
            P("pipe", "expert", None, "dp"),
            P("pipe", "expert", "dp", None),
        ),
        out_specs=P("pipe", None, "expert", "dp"),
        check_vma=False,
    )
```

```python
import jax
import jax.numpy as jnp
from jax import lax
from jax.sharding import PartitionSpec as P

TOP = 2
CAP = 16
AXES = ("dp", "pipe", "expert")
SMALL_GROUP = 8


class Ring:
    def __init__(self, n):
        self.n = n
        self.xor = n & (n - 1) == 0

    def ahead(self, me, s):
        return me ^ s if self.xor else (me + s) % self.n

    def behind(self, me, s):
        return me ^ s if self.xor else (me - s) % self.n

    def place(self, target, me):
        return target ^ me if self.xor else (target - me) % self.n


def build_maps(route_ids, route_gates, ring, me, rows_all):
    experts = ring.n
    flat_ids = route_ids.reshape(-1)
    onehot = (flat_ids[:, None] == jnp.arange(experts, dtype=jnp.int32)[None, :]).astype(jnp.int32)
    before = jnp.cumsum(onehot, axis=0) - onehot
    slot = jnp.sum(before * onehot, axis=1)
    placed = ring.place(flat_ids, me) * CAP + slot
    matches = jnp.arange(rows_all, dtype=jnp.int32)[:, None] == placed[None, :]
    dispatch_map = jnp.sum(matches.astype(jnp.float32).reshape(rows_all, -1, TOP), axis=2).astype(jnp.bfloat16)
    combine_map = jnp.sum(
        jnp.where(matches, route_gates.reshape(-1)[None, :], 0.0).reshape(rows_all, -1, TOP), axis=2
    )
    return dispatch_map, combine_map


def per_device(tokens, expert_ids, gates, w_gate, w_up, w_down):
    n_dp = lax.axis_size("dp")
    n_pipe = lax.axis_size("pipe")
    n_exp = lax.axis_size("expert")
    micro, tok_rows, width = tokens.shape
    units = w_gate.shape[3]
    columns = width // n_dp
    rows_all = n_exp * CAP
    d_me = lax.axis_index("dp")
    p_me = lax.axis_index("pipe")
    e_me = lax.axis_index("expert")
    dring = Ring(n_dp)
    ering = Ring(n_exp)
    small_dp = n_dp <= SMALL_GROUP

    def lin(d, p, e):
        return (d * n_pipe + p) * n_exp + e

    def expert_pairs(p, s, back):
        step = ering.behind if back else ering.ahead
        return [(lin(d, p, e), lin(d, p, step(e, s))) for d in range(n_dp) for e in range(n_exp)]

    def dp_pairs(p, s):
        return [(lin(d, p, e), lin(dring.ahead(d, s), p, e)) for d in range(n_dp) for e in range(n_exp)]

    relays = n_pipe == 2

    def relayed(chunks, p, target):
        q = 1 - p
        got = []
        for s in range(1, len(chunks) + 1):
            pairs = [(lin(d, p, e), lin(*target(d, e, s)[:1], q, *target(d, e, s)[1:])) for d in range(n_dp) for e in range(n_exp)]
            got.append(lax.ppermute(chunks[s - 1], AXES, pairs))
        handed = lax.ppermute(
            jnp.stack(got), AXES, [(lin(d, q, e), lin(d, p, e)) for d in range(n_dp) for e in range(n_exp)]
        )
        return [handed[i] for i in range(len(chunks))]

    gate_local = w_gate[0, 0]
    up_local = w_up[0, 0]
    down_local = w_down[0, 0]

    if small_dp:
        down_parts = []
        for s in range(n_dp):
            piece = lax.dynamic_slice_in_dim(down_local, dring.ahead(d_me, s) * columns, columns, 1)
            if s:
                piece = lax.ppermute(piece, "dp", [(i, dring.ahead(i, s)) for i in range(n_dp)])
            down_parts.append(piece)
        down_full = jnp.concatenate(down_parts, axis=0)
    else:
        down_full = lax.all_to_all(down_local, "dp", 1, 0, tiled=True)

    route_ids = expert_ids[0]
    route_gates = gates[0]
    maps = [build_maps(route_ids[m], route_gates[m], ering, e_me, rows_all) for m in range(micro)]
    dispatch_map = jnp.stack([mp[0] for mp in maps])
    combine_map = jnp.stack([mp[1] for mp in maps])

    def layer(current, p):
        outgoing = jnp.einsum("mrt,mtd->mrd", dispatch_map, current, preferred_element_type=jnp.float32)
        outgoing = outgoing.astype(jnp.bfloat16).reshape(micro, n_exp, CAP, width)
        if relays and ering.xor:
            arrived = [outgoing[:, 0]] + relayed(
                [outgoing[:, s] for s in range(1, n_exp)], p, lambda d, e, s: (d, ering.ahead(e, s))
            )
        else:
            arrived = [outgoing[:, 0]]
            for s in range(1, n_exp):
                arrived.append(lax.ppermute(outgoing[:, s], AXES, expert_pairs(p, s, False)))
        flat_rows = jnp.stack(arrived, axis=1).reshape(-1, width)
        squares = jnp.mean(jnp.square(flat_rows.astype(jnp.float32)), axis=1, keepdims=True)
        inv_rms = lax.rsqrt(squares + 1e-05)
        gate_act = jnp.dot(flat_rows, gate_local, preferred_element_type=jnp.float32) * inv_rms
        up_act = jnp.dot(flat_rows, up_local, preferred_element_type=jnp.float32) * inv_rms
        hidden = (jax.nn.silu(gate_act) * up_act).astype(jnp.bfloat16)
        if small_dp and relays and dring.xor:
            parts = [hidden] + relayed([hidden] * (n_dp - 1), p, lambda d, e, s: (dring.ahead(d, s), e))
            hidden_full = jnp.concatenate(parts, axis=1)
        elif small_dp:
            parts = [hidden]
            for s in range(1, n_dp):
                parts.append(lax.ppermute(hidden, AXES, dp_pairs(p, s)))
            hidden_full = jnp.concatenate(parts, axis=1)
        else:
            hidden_full = lax.all_gather(hidden, "dp", axis=1, tiled=True)
        expert_out = jnp.dot(hidden_full, down_full, preferred_element_type=jnp.float32).astype(jnp.bfloat16)
        expert_out = expert_out.reshape(micro, n_exp, CAP, columns)
        if relays and ering.xor:
            returned = [expert_out[:, 0]] + relayed(
                [expert_out[:, s] for s in range(1, n_exp)], p, lambda d, e, s: (d, ering.behind(e, s))
            )
        else:
            returned = [expert_out[:, 0]]
            for s in range(1, n_exp):
                returned.append(lax.ppermute(expert_out[:, s], AXES, expert_pairs(p, s, True)))
        returned = jnp.stack(returned, axis=1).reshape(micro, rows_all, columns)
        mixed = jnp.einsum(
            "mrt,mrc->mtc",
            combine_map,
            returned.astype(jnp.float32),
            precision=lax.Precision.HIGHEST,
            preferred_element_type=jnp.float32,
        )
        current_cols = lax.dynamic_slice_in_dim(current, d_me * columns, columns, 2)
        return (current_cols.astype(jnp.float32) + mixed).astype(jnp.bfloat16)

    current = tokens
    result = None
    for p in range(n_pipe):
        cols = layer(current, p)
        result = cols if result is None else jnp.where(p_me == p, cols, result)
        if p + 1 < n_pipe:
            if small_dp:
                parts = []
                for s in range(n_dp):
                    pairs = [
                        (lin(d, p, e), lin(dring.ahead(d, s), p + 1, e)) for d in range(n_dp) for e in range(n_exp)
                    ]
                    parts.append(lax.ppermute(cols, AXES, pairs))
                stacked = jnp.stack(parts)
                order = jnp.stack([dring.place(d_me, k) for k in range(n_dp)])
                stacked = jnp.take(stacked, order, axis=0)
                current = jnp.transpose(stacked, (1, 2, 0, 3)).reshape(micro, tok_rows, width)
            else:
                full = lax.all_gather(cols, "dp", axis=2, tiled=True)
                current = lax.ppermute(full, "pipe", [(p, p + 1)])
    return result[None]


def solution(mesh):
    return jax.shard_map(
        per_device,
        mesh=mesh,
        in_specs=(
            P(None, "expert", None),
            P("pipe", None, "expert", None),
            P("pipe", None, "expert", None),
            P("pipe", "expert", None, "dp"),
            P("pipe", "expert", None, "dp"),
            P("pipe", "expert", "dp", None),
        ),
        out_specs=P("pipe", None, "expert", "dp"),
        check_vma=False,
    )
```

```python
import jax
import jax.numpy as jnp
from jax import lax
from jax.sharding import PartitionSpec as P

TOP = 2
CAP = 16
AXES = ("dp", "pipe", "expert")
SMALL_GROUP = 8


class Ring:
    def __init__(self, n):
        self.n = n
        self.xor = n & (n - 1) == 0

    def ahead(self, me, s):
        return me ^ s if self.xor else (me + s) % self.n

    def behind(self, me, s):
        return me ^ s if self.xor else (me - s) % self.n

    def place(self, target, me):
        return target ^ me if self.xor else (target - me) % self.n


def build_maps(route_ids, route_gates, ring, me, rows_all):
    experts = ring.n
    flat_ids = route_ids.reshape(-1)
    onehot = (flat_ids[:, None] == jnp.arange(experts, dtype=jnp.int32)[None, :]).astype(jnp.int32)
    before = jnp.cumsum(onehot, axis=0) - onehot
    slot = jnp.sum(before * onehot, axis=1)
    placed = ring.place(flat_ids, me) * CAP + slot
    matches = jnp.arange(rows_all, dtype=jnp.int32)[:, None] == placed[None, :]
    dispatch_map = jnp.sum(matches.astype(jnp.float32).reshape(rows_all, -1, TOP), axis=2).astype(jnp.bfloat16)
    combine_map = jnp.sum(
        jnp.where(matches, route_gates.reshape(-1)[None, :], 0.0).reshape(rows_all, -1, TOP), axis=2
    )
    return dispatch_map, combine_map


def per_device(tokens, expert_ids, gates, w_gate, w_up, w_down):
    n_dp = lax.axis_size("dp")
    n_pipe = lax.axis_size("pipe")
    n_exp = lax.axis_size("expert")
    micro, tok_rows, width = tokens.shape
    units = w_gate.shape[3]
    columns = width // n_dp
    rows_all = n_exp * CAP
    d_me = lax.axis_index("dp")
    p_me = lax.axis_index("pipe")
    e_me = lax.axis_index("expert")
    dring = Ring(n_dp)
    ering = Ring(n_exp)
    small_dp = n_dp <= SMALL_GROUP

    def lin(d, p, e):
        return (d * n_pipe + p) * n_exp + e

    def expert_pairs(p, s, back):
        step = ering.behind if back else ering.ahead
        return [(lin(d, p, e), lin(d, p, step(e, s))) for d in range(n_dp) for e in range(n_exp)]

    def dp_pairs(p, s):
        return [(lin(d, p, e), lin(dring.ahead(d, s), p, e)) for d in range(n_dp) for e in range(n_exp)]

    gate_local = w_gate[0, 0]
    up_local = w_up[0, 0]
    down_local = w_down[0, 0]

    if small_dp:
        down_parts = []
        for s in range(n_dp):
            piece = lax.dynamic_slice_in_dim(down_local, dring.ahead(d_me, s) * columns, columns, 1)
            down_parts.append(piece)
        down_parts, tokens = lax.optimization_barrier((down_parts, tokens))
        for s in range(1, n_dp):
            down_parts[s] = lax.ppermute(down_parts[s], "dp", [(i, dring.ahead(i, s)) for i in range(n_dp)])
        down_full = jnp.concatenate(down_parts, axis=0)
    else:
        down_full = lax.all_to_all(down_local, "dp", 1, 0, tiled=True)

    route_ids = expert_ids[0]
    route_gates = gates[0]
    maps = [build_maps(route_ids[m], route_gates[m], ering, e_me, rows_all) for m in range(micro)]
    dispatch_map = jnp.stack([mp[0] for mp in maps])
    combine_map = jnp.stack([mp[1] for mp in maps])

    def layer(current, p):
        outgoing = jnp.einsum("mrt,mtd->mrd", dispatch_map, current, preferred_element_type=jnp.float32)
        outgoing = outgoing.astype(jnp.bfloat16).reshape(micro, n_exp, CAP, width)
        arrived = [outgoing[:, 0]]
        for s in range(1, n_exp):
            arrived.append(lax.ppermute(outgoing[:, s], AXES, expert_pairs(p, s, False)))
        flat_rows = jnp.stack(arrived, axis=1).reshape(-1, width)
        squares = jnp.mean(jnp.square(flat_rows.astype(jnp.float32)), axis=1, keepdims=True)
        inv_rms = lax.rsqrt(squares + 1e-05)
        gate_act = jnp.dot(flat_rows, gate_local, preferred_element_type=jnp.float32) * inv_rms
        up_act = jnp.dot(flat_rows, up_local, preferred_element_type=jnp.float32) * inv_rms
        hidden = (jax.nn.silu(gate_act) * up_act).astype(jnp.bfloat16)
        if small_dp:
            parts = [hidden]
            for s in range(1, n_dp):
                parts.append(lax.ppermute(hidden, AXES, dp_pairs(p, s)))
            hidden_full = jnp.concatenate(parts, axis=1)
        else:
            hidden_full = lax.all_gather(hidden, "dp", axis=1, tiled=True)
        expert_out = jnp.dot(hidden_full, down_full, preferred_element_type=jnp.float32).astype(jnp.bfloat16)
        expert_out = expert_out.reshape(micro, n_exp, CAP, columns)
        returned = [expert_out[:, 0]]
        for s in range(1, n_exp):
            returned.append(lax.ppermute(expert_out[:, s], AXES, expert_pairs(p, s, True)))
        returned = jnp.stack(returned, axis=1).reshape(micro, rows_all, columns)
        mixed = jnp.einsum(
            "mrt,mrc->mtc",
            combine_map,
            returned.astype(jnp.float32),
            precision=lax.Precision.HIGHEST,
            preferred_element_type=jnp.float32,
        )
        current_cols = lax.dynamic_slice_in_dim(current, d_me * columns, columns, 2)
        return (current_cols.astype(jnp.float32) + mixed).astype(jnp.bfloat16)

    current = tokens
    result = None
    for p in range(n_pipe):
        cols = layer(current, p)
        result = cols if result is None else jnp.where(p_me == p, cols, result)
        if p + 1 < n_pipe:
            if small_dp:
                parts = []
                for s in range(n_dp):
                    pairs = [
                        (lin(d, p, e), lin(dring.ahead(d, s), p + 1, e)) for d in range(n_dp) for e in range(n_exp)
                    ]
                    parts.append(lax.ppermute(cols, AXES, pairs))
                stacked = jnp.stack(parts)
                order = jnp.stack([dring.place(d_me, k) for k in range(n_dp)])
                stacked = jnp.take(stacked, order, axis=0)
                current = jnp.transpose(stacked, (1, 2, 0, 3)).reshape(micro, tok_rows, width)
            else:
                full = lax.all_gather(cols, "dp", axis=2, tiled=True)
                current = lax.ppermute(full, "pipe", [(p, p + 1)])
    return result[None]


def solution(mesh):
    return jax.shard_map(
        per_device,
        mesh=mesh,
        in_specs=(
            P(None, "expert", None),
            P("pipe", None, "expert", None),
            P("pipe", None, "expert", None),
            P("pipe", "expert", None, "dp"),
            P("pipe", "expert", None, "dp"),
            P("pipe", "expert", "dp", None),
        ),
        out_specs=P("pipe", None, "expert", "dp"),
        check_vma=False,
    )
```

```python
import jax
import jax.numpy as jnp
from jax import lax
from jax.sharding import PartitionSpec as P

TOP = 2
CAP = 16
AXES = ("dp", "pipe", "expert")
SMALL_GROUP = 8


class Ring:
    def __init__(self, n):
        self.n = n
        self.xor = n & (n - 1) == 0

    def ahead(self, me, s):
        return me ^ s if self.xor else (me + s) % self.n

    def behind(self, me, s):
        return me ^ s if self.xor else (me - s) % self.n

    def place(self, target, me):
        return target ^ me if self.xor else (target - me) % self.n


def build_maps(route_ids, route_gates, ring, me, rows_all):
    experts = ring.n
    flat_ids = route_ids.reshape(-1)
    onehot = (flat_ids[:, None] == jnp.arange(experts, dtype=jnp.int32)[None, :]).astype(jnp.int32)
    before = jnp.cumsum(onehot, axis=0) - onehot
    slot = jnp.sum(before * onehot, axis=1)
    placed = ring.place(flat_ids, me) * CAP + slot
    matches = jnp.arange(rows_all, dtype=jnp.int32)[:, None] == placed[None, :]
    dispatch_map = jnp.sum(matches.astype(jnp.float32).reshape(rows_all, -1, TOP), axis=2).astype(jnp.bfloat16)
    combine_map = jnp.sum(
        jnp.where(matches, route_gates.reshape(-1)[None, :], 0.0).reshape(rows_all, -1, TOP), axis=2
    )
    return dispatch_map, combine_map


def per_device(tokens, expert_ids, gates, w_gate, w_up, w_down):
    n_dp = lax.axis_size("dp")
    n_pipe = lax.axis_size("pipe")
    n_exp = lax.axis_size("expert")
    micro, tok_rows, width = tokens.shape
    units = w_gate.shape[3]
    columns = width // n_dp
    rows_all = n_exp * CAP
    d_me = lax.axis_index("dp")
    p_me = lax.axis_index("pipe")
    e_me = lax.axis_index("expert")
    dring = Ring(n_dp)
    ering = Ring(n_exp)
    small_dp = n_dp <= SMALL_GROUP

    def lin(d, p, e):
        return (d * n_pipe + p) * n_exp + e

    def expert_pairs(p, s, back):
        step = ering.behind if back else ering.ahead
        return [(lin(d, p, e), lin(d, p, step(e, s))) for d in range(n_dp) for e in range(n_exp)]

    def dp_pairs(p, s):
        return [(lin(d, p, e), lin(dring.ahead(d, s), p, e)) for d in range(n_dp) for e in range(n_exp)]

    gate_local = w_gate[0, 0]
    up_local = w_up[0, 0]
    down_local = w_down[0, 0]

    if small_dp:
        down_parts = []
        for s in range(n_dp):
            piece = lax.dynamic_slice_in_dim(down_local, dring.ahead(d_me, s) * columns, columns, 1)
            down_parts.append(piece)
        down_parts, tokens = lax.optimization_barrier((down_parts, tokens))
        for s in range(1, n_dp):
            down_parts[s] = lax.ppermute(down_parts[s], "dp", [(i, dring.ahead(i, s)) for i in range(n_dp)])
    else:
        down_full = lax.all_to_all(down_local, "dp", 1, 0, tiled=True)

    route_ids = expert_ids[0]
    route_gates = gates[0]
    maps = [build_maps(route_ids[m], route_gates[m], ering, e_me, rows_all) for m in range(micro)]
    dispatch_map = jnp.stack([mp[0] for mp in maps])
    combine_map = jnp.stack([mp[1] for mp in maps])

    def layer(current, p):
        outgoing = jnp.einsum("mrt,mtd->mrd", dispatch_map, current, preferred_element_type=jnp.float32)
        outgoing = outgoing.astype(jnp.bfloat16).reshape(micro, n_exp, CAP, width)
        arrived = [outgoing[:, 0]]
        for s in range(1, n_exp):
            arrived.append(lax.ppermute(outgoing[:, s], AXES, expert_pairs(p, s, False)))
        flat_rows = jnp.stack(arrived, axis=1).reshape(-1, width)
        squares = jnp.mean(jnp.square(flat_rows.astype(jnp.float32)), axis=1, keepdims=True)
        inv_rms = lax.rsqrt(squares + 1e-05)
        gate_act = jnp.dot(flat_rows, gate_local, preferred_element_type=jnp.float32) * inv_rms
        up_act = jnp.dot(flat_rows, up_local, preferred_element_type=jnp.float32) * inv_rms
        hidden = (jax.nn.silu(gate_act) * up_act).astype(jnp.bfloat16)
        if small_dp:
            parts = [hidden]
            for s in range(1, n_dp):
                parts.append(lax.ppermute(hidden, AXES, dp_pairs(p, s)))
            expert_out = jnp.dot(parts[0], down_parts[0], preferred_element_type=jnp.float32)
            for s in range(1, n_dp):
                expert_out = expert_out + jnp.dot(parts[s], down_parts[s], preferred_element_type=jnp.float32)
            expert_out = expert_out.astype(jnp.bfloat16)
        else:
            hidden_full = lax.all_gather(hidden, "dp", axis=1, tiled=True)
            expert_out = jnp.dot(hidden_full, down_full, preferred_element_type=jnp.float32).astype(jnp.bfloat16)
        expert_out = expert_out.reshape(micro, n_exp, CAP, columns)
        returned = [expert_out[:, 0]]
        for s in range(1, n_exp):
            returned.append(lax.ppermute(expert_out[:, s], AXES, expert_pairs(p, s, True)))
        returned = jnp.stack(returned, axis=1).reshape(micro, rows_all, columns)
        mixed = jnp.einsum(
            "mrt,mrc->mtc",
            combine_map,
            returned.astype(jnp.float32),
            precision=lax.Precision.HIGHEST,
            preferred_element_type=jnp.float32,
        )
        current_cols = lax.dynamic_slice_in_dim(current, d_me * columns, columns, 2)
        return (current_cols.astype(jnp.float32) + mixed).astype(jnp.bfloat16)

    current = tokens
    result = None
    for p in range(n_pipe):
        cols = layer(current, p)
        result = cols if result is None else jnp.where(p_me == p, cols, result)
        if p + 1 < n_pipe:
            if small_dp:
                parts = []
                for s in range(n_dp):
                    pairs = [
                        (lin(d, p, e), lin(dring.ahead(d, s), p + 1, e)) for d in range(n_dp) for e in range(n_exp)
                    ]
                    parts.append(lax.ppermute(cols, AXES, pairs))
                stacked = jnp.stack(parts)
                order = jnp.stack([dring.place(d_me, k) for k in range(n_dp)])
                stacked = jnp.take(stacked, order, axis=0)
                current = jnp.transpose(stacked, (1, 2, 0, 3)).reshape(micro, tok_rows, width)
            else:
                full = lax.all_gather(cols, "dp", axis=2, tiled=True)
                current = lax.ppermute(full, "pipe", [(p, p + 1)])
    return result[None]


def solution(mesh):
    return jax.shard_map(
        per_device,
        mesh=mesh,
        in_specs=(
            P(None, "expert", None),
            P("pipe", None, "expert", None),
            P("pipe", None, "expert", None),
            P("pipe", "expert", None, "dp"),
            P("pipe", "expert", None, "dp"),
            P("pipe", "expert", "dp", None),
        ),
        out_specs=P("pipe", None, "expert", "dp"),
        check_vma=False,
    )
```

```python
import jax
import jax.numpy as jnp
from jax import lax
from jax.sharding import PartitionSpec as P

TOP = 2
CAP = 16
AXES = ("dp", "pipe", "expert")
SMALL_GROUP = 8


class Ring:
    def __init__(self, n):
        self.n = n
        self.xor = n & (n - 1) == 0

    def ahead(self, me, s):
        return me ^ s if self.xor else (me + s) % self.n

    def behind(self, me, s):
        return me ^ s if self.xor else (me - s) % self.n

    def place(self, target, me):
        return target ^ me if self.xor else (target - me) % self.n


def build_maps(route_ids, route_gates, ring, me, rows_all):
    experts = ring.n
    flat_ids = route_ids.reshape(-1)
    onehot = (flat_ids[:, None] == jnp.arange(experts, dtype=jnp.int32)[None, :]).astype(jnp.int32)
    before = jnp.cumsum(onehot, axis=0) - onehot
    slot = jnp.sum(before * onehot, axis=1)
    placed = ring.place(flat_ids, me) * CAP + slot
    matches = jnp.arange(rows_all, dtype=jnp.int32)[:, None] == placed[None, :]
    dispatch_map = jnp.sum(matches.astype(jnp.float32).reshape(rows_all, -1, TOP), axis=2).astype(jnp.bfloat16)
    combine_map = jnp.sum(
        jnp.where(matches, route_gates.reshape(-1)[None, :], 0.0).reshape(rows_all, -1, TOP), axis=2
    )
    return dispatch_map, combine_map


def per_device(tokens, expert_ids, gates, w_gate, w_up, w_down):
    n_dp = lax.axis_size("dp")
    n_pipe = lax.axis_size("pipe")
    n_exp = lax.axis_size("expert")
    micro, tok_rows, width = tokens.shape
    units = w_gate.shape[3]
    columns = width // n_dp
    rows_all = n_exp * CAP
    d_me = lax.axis_index("dp")
    p_me = lax.axis_index("pipe")
    e_me = lax.axis_index("expert")
    dring = Ring(n_dp)
    ering = Ring(n_exp)
    small_dp = n_dp <= SMALL_GROUP

    def lin(d, p, e):
        return (d * n_pipe + p) * n_exp + e

    def expert_pairs(p, s, back):
        step = ering.behind if back else ering.ahead
        return [(lin(d, p, e), lin(d, p, step(e, s))) for d in range(n_dp) for e in range(n_exp)]

    def dp_pairs(p, s):
        return [(lin(d, p, e), lin(dring.ahead(d, s), p, e)) for d in range(n_dp) for e in range(n_exp)]

    gate_local = w_gate[0, 0]
    up_local = w_up[0, 0]
    down_local = w_down[0, 0]

    if small_dp:
        down_parts = []
        for s in range(n_dp):
            piece = lax.dynamic_slice_in_dim(down_local, dring.ahead(d_me, s) * columns, columns, 1)
            down_parts.append(piece)
        down_parts, tokens = lax.optimization_barrier((down_parts, tokens))
        for s in range(1, n_dp):
            down_parts[s] = lax.ppermute(down_parts[s], "dp", [(i, dring.ahead(i, s)) for i in range(n_dp)])
        down_full = jnp.concatenate(down_parts, axis=0)
    else:
        down_full = lax.all_to_all(down_local, "dp", 1, 0, tiled=True)

    route_ids = expert_ids[0]
    route_gates = gates[0]
    maps = [build_maps(route_ids[m], route_gates[m], ering, e_me, rows_all) for m in range(micro)]
    dispatch_map = jnp.stack([mp[0] for mp in maps])
    combine_map = jnp.stack([mp[1] for mp in maps])
    if ering.xor:
        combine_map = jnp.stack(
            [build_maps(route_ids[m], route_gates[m], ering, 0, rows_all)[1] for m in range(micro)]
        )

    def layer(current, p):
        outgoing = jnp.einsum("mrt,mtd->mrd", dispatch_map, current, preferred_element_type=jnp.float32)
        outgoing = outgoing.astype(jnp.bfloat16).reshape(micro, n_exp, CAP, width)
        arrived = [outgoing[:, 0]]
        for s in range(1, n_exp):
            arrived.append(lax.ppermute(outgoing[:, s], AXES, expert_pairs(p, s, False)))
        flat_rows = jnp.stack(arrived, axis=1).reshape(-1, width)
        squares = jnp.mean(jnp.square(flat_rows.astype(jnp.float32)), axis=1, keepdims=True)
        inv_rms = lax.rsqrt(squares + 1e-05)
        gate_act = jnp.dot(flat_rows, gate_local, preferred_element_type=jnp.float32) * inv_rms
        up_act = jnp.dot(flat_rows, up_local, preferred_element_type=jnp.float32) * inv_rms
        hidden = (jax.nn.silu(gate_act) * up_act).astype(jnp.bfloat16)
        if small_dp:
            parts = [hidden]
            for s in range(1, n_dp):
                parts.append(lax.ppermute(hidden, AXES, dp_pairs(p, s)))
            hidden_full = jnp.concatenate(parts, axis=1)
        else:
            hidden_full = lax.all_gather(hidden, "dp", axis=1, tiled=True)
        expert_out = jnp.dot(hidden_full, down_full, preferred_element_type=jnp.float32).astype(jnp.bfloat16)
        expert_out = expert_out.reshape(micro, n_exp, CAP, columns)
        if ering.xor:
            order = jnp.stack([ering.place(j, e_me) for j in range(n_exp)])
            by_block = jnp.take(expert_out, order, axis=1)
            returned = lax.all_to_all(by_block, "expert", 1, 1, tiled=True).reshape(micro, rows_all, columns)
        else:
            returned = [expert_out[:, 0]]
            for s in range(1, n_exp):
                returned.append(lax.ppermute(expert_out[:, s], AXES, expert_pairs(p, s, True)))
            returned = jnp.stack(returned, axis=1).reshape(micro, rows_all, columns)
        mixed = jnp.einsum(
            "mrt,mrc->mtc",
            combine_map,
            returned.astype(jnp.float32),
            precision=lax.Precision.HIGHEST,
            preferred_element_type=jnp.float32,
        )
        current_cols = lax.dynamic_slice_in_dim(current, d_me * columns, columns, 2)
        return (current_cols.astype(jnp.float32) + mixed).astype(jnp.bfloat16)

    current = tokens
    result = None
    for p in range(n_pipe):
        cols = layer(current, p)
        result = cols if result is None else jnp.where(p_me == p, cols, result)
        if p + 1 < n_pipe:
            if small_dp:
                parts = []
                for s in range(n_dp):
                    pairs = [
                        (lin(d, p, e), lin(dring.ahead(d, s), p + 1, e)) for d in range(n_dp) for e in range(n_exp)
                    ]
                    parts.append(lax.ppermute(cols, AXES, pairs))
                stacked = jnp.stack(parts)
                order = jnp.stack([dring.place(d_me, k) for k in range(n_dp)])
                stacked = jnp.take(stacked, order, axis=0)
                current = jnp.transpose(stacked, (1, 2, 0, 3)).reshape(micro, tok_rows, width)
            else:
                full = lax.all_gather(cols, "dp", axis=2, tiled=True)
                current = lax.ppermute(full, "pipe", [(p, p + 1)])
    return result[None]


def solution(mesh):
    return jax.shard_map(
        per_device,
        mesh=mesh,
        in_specs=(
            P(None, "expert", None),
            P("pipe", None, "expert", None),
            P("pipe", None, "expert", None),
            P("pipe", "expert", None, "dp"),
            P("pipe", "expert", None, "dp"),
            P("pipe", "expert", "dp", None),
        ),
        out_specs=P("pipe", None, "expert", "dp"),
        check_vma=False,
    )
```

```python
import jax
import jax.numpy as jnp
from jax import lax
from jax.sharding import PartitionSpec as P

TOP = 2
CAP = 16
AXES = ("dp", "pipe", "expert")
SMALL_GROUP = 8


class Ring:
    def __init__(self, n):
        self.n = n
        self.xor = n & (n - 1) == 0

    def ahead(self, me, s):
        return me ^ s if self.xor else (me + s) % self.n

    def behind(self, me, s):
        return me ^ s if self.xor else (me - s) % self.n

    def place(self, target, me):
        return target ^ me if self.xor else (target - me) % self.n


def build_maps(route_ids, route_gates, ring, me, rows_all):
    experts = ring.n
    flat_ids = route_ids.reshape(-1)
    onehot = (flat_ids[:, None] == jnp.arange(experts, dtype=jnp.int32)[None, :]).astype(jnp.int32)
    before = jnp.cumsum(onehot, axis=0) - onehot
    slot = jnp.sum(before * onehot, axis=1)
    placed = ring.place(flat_ids, me) * CAP + slot
    matches = jnp.arange(rows_all, dtype=jnp.int32)[:, None] == placed[None, :]
    dispatch_map = jnp.sum(matches.astype(jnp.float32).reshape(rows_all, -1, TOP), axis=2).astype(jnp.bfloat16)
    combine_map = jnp.sum(
        jnp.where(matches, route_gates.reshape(-1)[None, :], 0.0).reshape(rows_all, -1, TOP), axis=2
    )
    return dispatch_map, combine_map


def per_device(tokens, expert_ids, gates, w_gate, w_up, w_down):
    n_dp = lax.axis_size("dp")
    n_pipe = lax.axis_size("pipe")
    n_exp = lax.axis_size("expert")
    micro, tok_rows, width = tokens.shape
    units = w_gate.shape[3]
    columns = width // n_dp
    rows_all = n_exp * CAP
    d_me = lax.axis_index("dp")
    p_me = lax.axis_index("pipe")
    e_me = lax.axis_index("expert")
    dring = Ring(n_dp)
    ering = Ring(n_exp)
    small_dp = n_dp <= SMALL_GROUP

    def lin(d, p, e):
        return (d * n_pipe + p) * n_exp + e

    def expert_pairs(p, s, back):
        step = ering.behind if back else ering.ahead
        return [(lin(d, p, e), lin(d, p, step(e, s))) for d in range(n_dp) for e in range(n_exp)]

    def dp_pairs(p, s):
        return [(lin(d, p, e), lin(dring.ahead(d, s), p, e)) for d in range(n_dp) for e in range(n_exp)]

    gate_local = w_gate[0, 0]
    up_local = w_up[0, 0]
    down_local = w_down[0, 0]

    if small_dp:
        down_parts = []
        for s in range(n_dp):
            piece = lax.dynamic_slice_in_dim(down_local, dring.ahead(d_me, s) * columns, columns, 1)
            down_parts.append(piece)
        down_parts, tokens = lax.optimization_barrier((down_parts, tokens))
        for s in range(1, n_dp):
            down_parts[s] = lax.ppermute(down_parts[s], "dp", [(i, dring.ahead(i, s)) for i in range(n_dp)])
        down_full = jnp.concatenate(down_parts, axis=0)
    else:
        down_full = lax.all_to_all(down_local, "dp", 1, 0, tiled=True)

    route_ids = expert_ids[0]
    route_gates = gates[0]
    maps = [build_maps(route_ids[m], route_gates[m], ering, e_me, rows_all) for m in range(micro)]
    dispatch_map = jnp.stack([mp[0] for mp in maps])
    combine_map = jnp.stack([mp[1] for mp in maps])
    if ering.xor:
        maps = [build_maps(route_ids[m], route_gates[m], ering, 0, rows_all) for m in range(micro)]
        dispatch_map = jnp.stack([mp[0] for mp in maps])
        combine_map = jnp.stack([mp[1] for mp in maps])

    def layer(current, p):
        outgoing = jnp.einsum("mrt,mtd->mrd", dispatch_map, current, preferred_element_type=jnp.float32)
        outgoing = outgoing.astype(jnp.bfloat16).reshape(micro, n_exp, CAP, width)
        if ering.xor:
            flat_rows = lax.all_to_all(outgoing, "expert", 1, 1, tiled=True).reshape(-1, width)
        else:
            arrived = [outgoing[:, 0]]
            for s in range(1, n_exp):
                arrived.append(lax.ppermute(outgoing[:, s], AXES, expert_pairs(p, s, False)))
            flat_rows = jnp.stack(arrived, axis=1).reshape(-1, width)
        squares = jnp.mean(jnp.square(flat_rows.astype(jnp.float32)), axis=1, keepdims=True)
        inv_rms = lax.rsqrt(squares + 1e-05)
        gate_act = jnp.dot(flat_rows, gate_local, preferred_element_type=jnp.float32) * inv_rms
        up_act = jnp.dot(flat_rows, up_local, preferred_element_type=jnp.float32) * inv_rms
        hidden = (jax.nn.silu(gate_act) * up_act).astype(jnp.bfloat16)
        if small_dp:
            parts = [hidden]
            for s in range(1, n_dp):
                parts.append(lax.ppermute(hidden, AXES, dp_pairs(p, s)))
            hidden_full = jnp.concatenate(parts, axis=1)
        else:
            hidden_full = lax.all_gather(hidden, "dp", axis=1, tiled=True)
        expert_out = jnp.dot(hidden_full, down_full, preferred_element_type=jnp.float32).astype(jnp.bfloat16)
        expert_out = expert_out.reshape(micro, n_exp, CAP, columns)
        if ering.xor:
            returned = lax.all_to_all(expert_out, "expert", 1, 1, tiled=True).reshape(micro, rows_all, columns)
        else:
            returned = [expert_out[:, 0]]
            for s in range(1, n_exp):
                returned.append(lax.ppermute(expert_out[:, s], AXES, expert_pairs(p, s, True)))
            returned = jnp.stack(returned, axis=1).reshape(micro, rows_all, columns)
        mixed = jnp.einsum(
            "mrt,mrc->mtc",
            combine_map,
            returned.astype(jnp.float32),
            precision=lax.Precision.HIGHEST,
            preferred_element_type=jnp.float32,
        )
        current_cols = lax.dynamic_slice_in_dim(current, d_me * columns, columns, 2)
        return (current_cols.astype(jnp.float32) + mixed).astype(jnp.bfloat16)

    current = tokens
    result = None
    for p in range(n_pipe):
        cols = layer(current, p)
        result = cols if result is None else jnp.where(p_me == p, cols, result)
        if p + 1 < n_pipe:
            if small_dp:
                parts = []
                for s in range(n_dp):
                    pairs = [
                        (lin(d, p, e), lin(dring.ahead(d, s), p + 1, e)) for d in range(n_dp) for e in range(n_exp)
                    ]
                    parts.append(lax.ppermute(cols, AXES, pairs))
                stacked = jnp.stack(parts)
                order = jnp.stack([dring.place(d_me, k) for k in range(n_dp)])
                stacked = jnp.take(stacked, order, axis=0)
                current = jnp.transpose(stacked, (1, 2, 0, 3)).reshape(micro, tok_rows, width)
            else:
                full = lax.all_gather(cols, "dp", axis=2, tiled=True)
                current = lax.ppermute(full, "pipe", [(p, p + 1)])
    return result[None]


def solution(mesh):
    return jax.shard_map(
        per_device,
        mesh=mesh,
        in_specs=(
            P(None, "expert", None),
            P("pipe", None, "expert", None),
            P("pipe", None, "expert", None),
            P("pipe", "expert", None, "dp"),
            P("pipe", "expert", None, "dp"),
            P("pipe", "expert", "dp", None),
        ),
        out_specs=P("pipe", None, "expert", "dp"),
        check_vma=False,
    )
```

```python
import jax
import jax.numpy as jnp
from jax import lax
from jax.sharding import PartitionSpec as P

TOP = 2
CAP = 16
AXES = ("dp", "pipe", "expert")
SMALL_GROUP = 8


class Ring:
    def __init__(self, n):
        self.n = n
        self.xor = n & (n - 1) == 0

    def ahead(self, me, s):
        return me ^ s if self.xor else (me + s) % self.n

    def behind(self, me, s):
        return me ^ s if self.xor else (me - s) % self.n

    def place(self, target, me):
        return target ^ me if self.xor else (target - me) % self.n


def build_maps(route_ids, route_gates, ring, me, rows_all):
    experts = ring.n
    flat_ids = route_ids.reshape(-1)
    onehot = (flat_ids[:, None] == jnp.arange(experts, dtype=jnp.int32)[None, :]).astype(jnp.int32)
    before = jnp.cumsum(onehot, axis=0) - onehot
    slot = jnp.sum(before * onehot, axis=1)
    placed = ring.place(flat_ids, me) * CAP + slot
    matches = jnp.arange(rows_all, dtype=jnp.int32)[:, None] == placed[None, :]
    dispatch_map = jnp.sum(matches.astype(jnp.float32).reshape(rows_all, -1, TOP), axis=2).astype(jnp.bfloat16)
    combine_map = jnp.sum(
        jnp.where(matches, route_gates.reshape(-1)[None, :], 0.0).reshape(rows_all, -1, TOP), axis=2
    )
    return dispatch_map, combine_map


def per_device(tokens, expert_ids, gates, w_gate, w_up, w_down):
    n_dp = lax.axis_size("dp")
    n_pipe = lax.axis_size("pipe")
    n_exp = lax.axis_size("expert")
    micro, tok_rows, width = tokens.shape
    units = w_gate.shape[3]
    columns = width // n_dp
    rows_all = n_exp * CAP
    d_me = lax.axis_index("dp")
    p_me = lax.axis_index("pipe")
    e_me = lax.axis_index("expert")
    dring = Ring(n_dp)
    ering = Ring(n_exp)
    small_dp = n_dp <= SMALL_GROUP

    def lin(d, p, e):
        return (d * n_pipe + p) * n_exp + e

    def expert_pairs(p, s, back):
        step = ering.behind if back else ering.ahead
        return [(lin(d, p, e), lin(d, p, step(e, s))) for d in range(n_dp) for e in range(n_exp)]

    def dp_pairs(p, s):
        return [(lin(d, p, e), lin(dring.ahead(d, s), p, e)) for d in range(n_dp) for e in range(n_exp)]

    gate_local = w_gate[0, 0]
    up_local = w_up[0, 0]
    down_local = w_down[0, 0]

    if small_dp:
        down_parts = []
        for s in range(n_dp):
            piece = lax.dynamic_slice_in_dim(down_local, dring.ahead(d_me, s) * columns, columns, 1)
            down_parts.append(piece)
        down_parts, tokens = lax.optimization_barrier((down_parts, tokens))
        for s in range(1, n_dp):
            down_parts[s] = lax.ppermute(down_parts[s], "dp", [(i, dring.ahead(i, s)) for i in range(n_dp)])
        down_full = jnp.concatenate(down_parts, axis=0)
    else:
        down_full = lax.all_to_all(down_local, "dp", 1, 0, tiled=True)

    route_ids = expert_ids[0]
    route_gates = gates[0]
    maps = [build_maps(route_ids[m], route_gates[m], ering, e_me, rows_all) for m in range(micro)]
    dispatch_map = jnp.stack([mp[0] for mp in maps])
    combine_map = jnp.stack([mp[1] for mp in maps])
    if ering.xor:
        combine_map = jnp.stack(
            [build_maps(route_ids[m], route_gates[m], ering, 0, rows_all)[1] for m in range(micro)]
        )

    def layer(current, p):
        outgoing = jnp.einsum("mrt,mtd->mrd", dispatch_map, current, preferred_element_type=jnp.float32)
        outgoing = outgoing.astype(jnp.bfloat16).reshape(micro, n_exp, CAP, width)
        arrived = [outgoing[:, 0]]
        for s in range(1, n_exp):
            arrived.append(lax.ppermute(outgoing[:, s], AXES, expert_pairs(p, s, False)))
        flat_rows = jnp.stack(arrived, axis=1).reshape(-1, width)
        down_use = down_full
        if p == 0:
            down_use, flat_rows = lax.optimization_barrier((down_full, flat_rows))
        squares = jnp.mean(jnp.square(flat_rows.astype(jnp.float32)), axis=1, keepdims=True)
        inv_rms = lax.rsqrt(squares + 1e-05)
        gate_act = jnp.dot(flat_rows, gate_local, preferred_element_type=jnp.float32) * inv_rms
        up_act = jnp.dot(flat_rows, up_local, preferred_element_type=jnp.float32) * inv_rms
        hidden = (jax.nn.silu(gate_act) * up_act).astype(jnp.bfloat16)
        if small_dp:
            parts = [hidden]
            for s in range(1, n_dp):
                parts.append(lax.ppermute(hidden, AXES, dp_pairs(p, s)))
            hidden_full = jnp.concatenate(parts, axis=1)
        else:
            hidden_full = lax.all_gather(hidden, "dp", axis=1, tiled=True)
        expert_out = jnp.dot(hidden_full, down_use, preferred_element_type=jnp.float32).astype(jnp.bfloat16)
        expert_out = expert_out.reshape(micro, n_exp, CAP, columns)
        if ering.xor:
            order = jnp.stack([ering.place(j, e_me) for j in range(n_exp)])
            by_block = jnp.take(expert_out, order, axis=1)
            returned = lax.all_to_all(by_block, "expert", 1, 1, tiled=True).reshape(micro, rows_all, columns)
        else:
            returned = [expert_out[:, 0]]
            for s in range(1, n_exp):
                returned.append(lax.ppermute(expert_out[:, s], AXES, expert_pairs(p, s, True)))
            returned = jnp.stack(returned, axis=1).reshape(micro, rows_all, columns)
        mixed = jnp.einsum(
            "mrt,mrc->mtc",
            combine_map,
            returned.astype(jnp.float32),
            precision=lax.Precision.HIGHEST,
            preferred_element_type=jnp.float32,
        )
        current_cols = lax.dynamic_slice_in_dim(current, d_me * columns, columns, 2)
        return (current_cols.astype(jnp.float32) + mixed).astype(jnp.bfloat16)

    current = tokens
    result = None
    for p in range(n_pipe):
        cols = layer(current, p)
        result = cols if result is None else jnp.where(p_me == p, cols, result)
        if p + 1 < n_pipe:
            if small_dp:
                parts = []
                for s in range(n_dp):
                    pairs = [
                        (lin(d, p, e), lin(dring.ahead(d, s), p + 1, e)) for d in range(n_dp) for e in range(n_exp)
                    ]
                    parts.append(lax.ppermute(cols, AXES, pairs))
                stacked = jnp.stack(parts)
                order = jnp.stack([dring.place(d_me, k) for k in range(n_dp)])
                stacked = jnp.take(stacked, order, axis=0)
                current = jnp.transpose(stacked, (1, 2, 0, 3)).reshape(micro, tok_rows, width)
            else:
                full = lax.all_gather(cols, "dp", axis=2, tiled=True)
                current = lax.ppermute(full, "pipe", [(p, p + 1)])
    return result[None]


def solution(mesh):
    return jax.shard_map(
        per_device,
        mesh=mesh,
        in_specs=(
            P(None, "expert", None),
            P("pipe", None, "expert", None),
            P("pipe", None, "expert", None),
            P("pipe", "expert", None, "dp"),
            P("pipe", "expert", None, "dp"),
            P("pipe", "expert", "dp", None),
        ),
        out_specs=P("pipe", None, "expert", "dp"),
        check_vma=False,
    )
```

```python
import jax
import jax.numpy as jnp
from jax import lax
from jax.sharding import PartitionSpec as P

TOP = 2
CAP = 16
AXES = ("dp", "pipe", "expert")
SMALL_GROUP = 8


class Ring:
    def __init__(self, n):
        self.n = n
        self.xor = n & (n - 1) == 0

    def ahead(self, me, s):
        return me ^ s if self.xor else (me + s) % self.n

    def behind(self, me, s):
        return me ^ s if self.xor else (me - s) % self.n

    def place(self, target, me):
        return target ^ me if self.xor else (target - me) % self.n


def build_maps(route_ids, route_gates, ring, me, rows_all):
    experts = ring.n
    flat_ids = route_ids.reshape(-1)
    onehot = (flat_ids[:, None] == jnp.arange(experts, dtype=jnp.int32)[None, :]).astype(jnp.int32)
    before = jnp.cumsum(onehot, axis=0) - onehot
    slot = jnp.sum(before * onehot, axis=1)
    placed = ring.place(flat_ids, me) * CAP + slot
    matches = jnp.arange(rows_all, dtype=jnp.int32)[:, None] == placed[None, :]
    dispatch_map = jnp.sum(matches.astype(jnp.float32).reshape(rows_all, -1, TOP), axis=2).astype(jnp.bfloat16)
    combine_map = jnp.sum(
        jnp.where(matches, route_gates.reshape(-1)[None, :], 0.0).reshape(rows_all, -1, TOP), axis=2
    )
    return dispatch_map, combine_map


def per_device(tokens, expert_ids, gates, w_gate, w_up, w_down):
    n_dp = lax.axis_size("dp")
    n_pipe = lax.axis_size("pipe")
    n_exp = lax.axis_size("expert")
    micro, tok_rows, width = tokens.shape
    units = w_gate.shape[3]
    columns = width // n_dp
    rows_all = n_exp * CAP
    d_me = lax.axis_index("dp")
    p_me = lax.axis_index("pipe")
    e_me = lax.axis_index("expert")
    dring = Ring(n_dp)
    ering = Ring(n_exp)
    small_dp = n_dp <= SMALL_GROUP

    def lin(d, p, e):
        return (d * n_pipe + p) * n_exp + e

    def expert_pairs(p, s, back):
        step = ering.behind if back else ering.ahead
        return [(lin(d, p, e), lin(d, p, step(e, s))) for d in range(n_dp) for e in range(n_exp)]

    def dp_pairs(p, s):
        return [(lin(d, p, e), lin(dring.ahead(d, s), p, e)) for d in range(n_dp) for e in range(n_exp)]

    gate_local = w_gate[0, 0]
    up_local = w_up[0, 0]
    down_local = w_down[0, 0]

    down_full = lax.all_to_all(down_local, "dp", 1, 0, tiled=True)
    if small_dp:
        order = jnp.stack([dring.behind(d_me, s) for s in range(n_dp)])
        down_full = jnp.take(down_full.reshape(n_dp, units, columns), order, axis=0).reshape(n_dp * units, columns)

    route_ids = expert_ids[0]
    route_gates = gates[0]
    maps = [build_maps(route_ids[m], route_gates[m], ering, e_me, rows_all) for m in range(micro)]
    dispatch_map = jnp.stack([mp[0] for mp in maps])
    combine_map = jnp.stack([mp[1] for mp in maps])
    if ering.xor:
        combine_map = jnp.stack(
            [build_maps(route_ids[m], route_gates[m], ering, 0, rows_all)[1] for m in range(micro)]
        )

    def layer(current, p):
        outgoing = jnp.einsum("mrt,mtd->mrd", dispatch_map, current, preferred_element_type=jnp.float32)
        outgoing = outgoing.astype(jnp.bfloat16).reshape(micro, n_exp, CAP, width)
        arrived = [outgoing[:, 0]]
        for s in range(1, n_exp):
            arrived.append(lax.ppermute(outgoing[:, s], AXES, expert_pairs(p, s, False)))
        flat_rows = jnp.stack(arrived, axis=1).reshape(-1, width)
        squares = jnp.mean(jnp.square(flat_rows.astype(jnp.float32)), axis=1, keepdims=True)
        inv_rms = lax.rsqrt(squares + 1e-05)
        gate_act = jnp.dot(flat_rows, gate_local, preferred_element_type=jnp.float32) * inv_rms
        up_act = jnp.dot(flat_rows, up_local, preferred_element_type=jnp.float32) * inv_rms
        hidden = (jax.nn.silu(gate_act) * up_act).astype(jnp.bfloat16)
        if small_dp:
            parts = [hidden]
            for s in range(1, n_dp):
                parts.append(lax.ppermute(hidden, AXES, dp_pairs(p, s)))
            hidden_full = jnp.concatenate(parts, axis=1)
        else:
            hidden_full = lax.all_gather(hidden, "dp", axis=1, tiled=True)
        expert_out = jnp.dot(hidden_full, down_full, preferred_element_type=jnp.float32).astype(jnp.bfloat16)
        expert_out = expert_out.reshape(micro, n_exp, CAP, columns)
        if ering.xor:
            order = jnp.stack([ering.place(j, e_me) for j in range(n_exp)])
            by_block = jnp.take(expert_out, order, axis=1)
            returned = lax.all_to_all(by_block, "expert", 1, 1, tiled=True).reshape(micro, rows_all, columns)
        else:
            returned = [expert_out[:, 0]]
            for s in range(1, n_exp):
                returned.append(lax.ppermute(expert_out[:, s], AXES, expert_pairs(p, s, True)))
            returned = jnp.stack(returned, axis=1).reshape(micro, rows_all, columns)
        mixed = jnp.einsum(
            "mrt,mrc->mtc",
            combine_map,
            returned.astype(jnp.float32),
            precision=lax.Precision.HIGHEST,
            preferred_element_type=jnp.float32,
        )
        current_cols = lax.dynamic_slice_in_dim(current, d_me * columns, columns, 2)
        return (current_cols.astype(jnp.float32) + mixed).astype(jnp.bfloat16)

    current = tokens
    result = None
    for p in range(n_pipe):
        cols = layer(current, p)
        result = cols if result is None else jnp.where(p_me == p, cols, result)
        if p + 1 < n_pipe:
            if small_dp:
                parts = []
                for s in range(n_dp):
                    pairs = [
                        (lin(d, p, e), lin(dring.ahead(d, s), p + 1, e)) for d in range(n_dp) for e in range(n_exp)
                    ]
                    parts.append(lax.ppermute(cols, AXES, pairs))
                stacked = jnp.stack(parts)
                order = jnp.stack([dring.place(d_me, k) for k in range(n_dp)])
                stacked = jnp.take(stacked, order, axis=0)
                current = jnp.transpose(stacked, (1, 2, 0, 3)).reshape(micro, tok_rows, width)
            else:
                full = lax.all_gather(cols, "dp", axis=2, tiled=True)
                current = lax.ppermute(full, "pipe", [(p, p + 1)])
    return result[None]


def solution(mesh):
    return jax.shard_map(
        per_device,
        mesh=mesh,
        in_specs=(
            P(None, "expert", None),
            P("pipe", None, "expert", None),
            P("pipe", None, "expert", None),
            P("pipe", "expert", None, "dp"),
            P("pipe", "expert", None, "dp"),
            P("pipe", "expert", "dp", None),
        ),
        out_specs=P("pipe", None, "expert", "dp"),
        check_vma=False,
    )
```

```python
import jax
import jax.numpy as jnp
from jax import lax
from jax.sharding import PartitionSpec as P

TOP = 2
CAP = 16
AXES = ("dp", "pipe", "expert")
SMALL_GROUP = 8


class Ring:
    def __init__(self, n):
        self.n = n
        self.xor = n & (n - 1) == 0

    def ahead(self, me, s):
        return me ^ s if self.xor else (me + s) % self.n

    def behind(self, me, s):
        return me ^ s if self.xor else (me - s) % self.n

    def place(self, target, me):
        return target ^ me if self.xor else (target - me) % self.n


def build_maps(route_ids, route_gates, ring, me, rows_all):
    experts = ring.n
    flat_ids = route_ids.reshape(-1)
    onehot = (flat_ids[:, None] == jnp.arange(experts, dtype=jnp.int32)[None, :]).astype(jnp.int32)
    before = jnp.cumsum(onehot, axis=0) - onehot
    slot = jnp.sum(before * onehot, axis=1)
    placed = ring.place(flat_ids, me) * CAP + slot
    matches = jnp.arange(rows_all, dtype=jnp.int32)[:, None] == placed[None, :]
    dispatch_map = jnp.sum(matches.astype(jnp.float32).reshape(rows_all, -1, TOP), axis=2).astype(jnp.bfloat16)
    combine_map = jnp.sum(
        jnp.where(matches, route_gates.reshape(-1)[None, :], 0.0).reshape(rows_all, -1, TOP), axis=2
    )
    return dispatch_map, combine_map


def per_device(tokens, expert_ids, gates, w_gate, w_up, w_down):
    n_dp = lax.axis_size("dp")
    n_pipe = lax.axis_size("pipe")
    n_exp = lax.axis_size("expert")
    micro, tok_rows, width = tokens.shape
    units = w_gate.shape[3]
    columns = width // n_dp
    rows_all = n_exp * CAP
    d_me = lax.axis_index("dp")
    p_me = lax.axis_index("pipe")
    e_me = lax.axis_index("expert")
    dring = Ring(n_dp)
    ering = Ring(n_exp)
    small_dp = n_dp <= SMALL_GROUP

    def lin(d, p, e):
        return (d * n_pipe + p) * n_exp + e

    def expert_pairs(p, s, back):
        step = ering.behind if back else ering.ahead
        return [(lin(d, p, e), lin(d, p, step(e, s))) for d in range(n_dp) for e in range(n_exp)]

    def dp_pairs(p, s):
        return [(lin(d, p, e), lin(dring.ahead(d, s), p, e)) for d in range(n_dp) for e in range(n_exp)]

    gate_local = w_gate[0, 0]
    up_local = w_up[0, 0]
    down_local = w_down[0, 0]

    def resplit_down(p, anchor):
        if not small_dp:
            return lax.all_to_all(down_local, "dp", 1, 0, tiled=True), anchor
        parts = [lax.dynamic_slice_in_dim(down_local, dring.ahead(d_me, s) * columns, columns, 1) for s in range(n_dp)]
        parts, anchor = lax.optimization_barrier((parts, anchor))
        for s in range(1, n_dp):
            parts[s] = lax.ppermute(parts[s], AXES, dp_pairs(p, s))
        return jnp.concatenate(parts, axis=0), anchor

    down_full = {}
    down_full[0], tokens = resplit_down(0, tokens)

    route_ids = expert_ids[0]
    route_gates = gates[0]
    maps = [build_maps(route_ids[m], route_gates[m], ering, e_me, rows_all) for m in range(micro)]
    dispatch_map = jnp.stack([mp[0] for mp in maps])
    combine_map = jnp.stack([mp[1] for mp in maps])
    absolute_dispatch = dispatch_map
    if ering.xor:
        maps = [build_maps(route_ids[m], route_gates[m], ering, 0, rows_all) for m in range(micro)]
        absolute_dispatch = jnp.stack([mp[0] for mp in maps])
        combine_map = jnp.stack([mp[1] for mp in maps])

    def layer(current, p):
        if p == 0 and ering.xor:
            outgoing = jnp.einsum("mrt,mtd->mrd", absolute_dispatch, current, preferred_element_type=jnp.float32)
            outgoing = outgoing.astype(jnp.bfloat16).reshape(micro, n_exp, CAP, width)
            flat_rows = lax.all_to_all(outgoing, "expert", 1, 1, tiled=True).reshape(-1, width)
            in_block_order = True
        else:
            outgoing = jnp.einsum("mrt,mtd->mrd", dispatch_map, current, preferred_element_type=jnp.float32)
            outgoing = outgoing.astype(jnp.bfloat16).reshape(micro, n_exp, CAP, width)
            arrived = [outgoing[:, 0]]
            for s in range(1, n_exp):
                arrived.append(lax.ppermute(outgoing[:, s], AXES, expert_pairs(p, s, False)))
            flat_rows = jnp.stack(arrived, axis=1).reshape(-1, width)
            in_block_order = False
        squares = jnp.mean(jnp.square(flat_rows.astype(jnp.float32)), axis=1, keepdims=True)
        inv_rms = lax.rsqrt(squares + 1e-05)
        gate_act = jnp.dot(flat_rows, gate_local, preferred_element_type=jnp.float32) * inv_rms
        up_act = jnp.dot(flat_rows, up_local, preferred_element_type=jnp.float32) * inv_rms
        hidden = (jax.nn.silu(gate_act) * up_act).astype(jnp.bfloat16)
        if small_dp:
            parts = [hidden]
            for s in range(1, n_dp):
                parts.append(lax.ppermute(hidden, AXES, dp_pairs(p, s)))
            hidden_full = jnp.concatenate(parts, axis=1)
        else:
            hidden_full = lax.all_gather(hidden, "dp", axis=1, tiled=True)
        expert_out = jnp.dot(hidden_full, down_full[p], preferred_element_type=jnp.float32).astype(jnp.bfloat16)
        expert_out = expert_out.reshape(micro, n_exp, CAP, columns)
        if ering.xor:
            if in_block_order:
                by_block = expert_out
            else:
                order = jnp.stack([ering.place(j, e_me) for j in range(n_exp)])
                by_block = jnp.take(expert_out, order, axis=1)
            returned = lax.all_to_all(by_block, "expert", 1, 1, tiled=True).reshape(micro, rows_all, columns)
        else:
            returned = [expert_out[:, 0]]
            for s in range(1, n_exp):
                returned.append(lax.ppermute(expert_out[:, s], AXES, expert_pairs(p, s, True)))
            returned = jnp.stack(returned, axis=1).reshape(micro, rows_all, columns)
        mixed = jnp.einsum(
            "mrt,mrc->mtc",
            combine_map,
            returned.astype(jnp.float32),
            precision=lax.Precision.HIGHEST,
            preferred_element_type=jnp.float32,
        )
        current_cols = lax.dynamic_slice_in_dim(current, d_me * columns, columns, 2)
        return (current_cols.astype(jnp.float32) + mixed).astype(jnp.bfloat16)

    current = tokens
    result = None
    for p in range(n_pipe):
        cols = layer(current, p)
        if p + 1 < n_pipe:
            down_full[p + 1], cols = resplit_down(p + 1, cols)
            down_full[p + 1], cols = lax.optimization_barrier((down_full[p + 1], cols))
        result = cols if result is None else jnp.where(p_me == p, cols, result)
        if p + 1 < n_pipe:
            if small_dp:
                parts = []
                for s in range(n_dp):
                    pairs = [
                        (lin(d, p, e), lin(dring.ahead(d, s), p + 1, e)) for d in range(n_dp) for e in range(n_exp)
                    ]
                    parts.append(lax.ppermute(cols, AXES, pairs))
                stacked = jnp.stack(parts)
                order = jnp.stack([dring.place(d_me, k) for k in range(n_dp)])
                stacked = jnp.take(stacked, order, axis=0)
                current = jnp.transpose(stacked, (1, 2, 0, 3)).reshape(micro, tok_rows, width)
            else:
                full = lax.all_gather(cols, "dp", axis=2, tiled=True)
                current = lax.ppermute(full, "pipe", [(p, p + 1)])
    return result[None]


def solution(mesh):
    return jax.shard_map(
        per_device,
        mesh=mesh,
        in_specs=(
            P(None, "expert", None),
            P("pipe", None, "expert", None),
            P("pipe", None, "expert", None),
            P("pipe", "expert", None, "dp"),
            P("pipe", "expert", None, "dp"),
            P("pipe", "expert", "dp", None),
        ),
        out_specs=P("pipe", None, "expert", "dp"),
        check_vma=False,
    )
```

```python
import jax
import jax.numpy as jnp
from jax import lax
from jax.sharding import PartitionSpec as P

TOP = 2
CAP = 16
AXES = ("dp", "pipe", "expert")
SMALL_GROUP = 8


class Ring:
    def __init__(self, n):
        self.n = n
        self.xor = n & (n - 1) == 0

    def ahead(self, me, s):
        return me ^ s if self.xor else (me + s) % self.n

    def behind(self, me, s):
        return me ^ s if self.xor else (me - s) % self.n

    def place(self, target, me):
        return target ^ me if self.xor else (target - me) % self.n


def build_maps(route_ids, route_gates, ring, me, rows_all):
    experts = ring.n
    flat_ids = route_ids.reshape(-1)
    onehot = (flat_ids[:, None] == jnp.arange(experts, dtype=jnp.int32)[None, :]).astype(jnp.int32)
    before = jnp.cumsum(onehot, axis=0) - onehot
    slot = jnp.sum(before * onehot, axis=1)
    placed = ring.place(flat_ids, me) * CAP + slot
    matches = jnp.arange(rows_all, dtype=jnp.int32)[:, None] == placed[None, :]
    dispatch_map = jnp.sum(matches.astype(jnp.float32).reshape(rows_all, -1, TOP), axis=2).astype(jnp.bfloat16)
    combine_map = jnp.sum(
        jnp.where(matches, route_gates.reshape(-1)[None, :], 0.0).reshape(rows_all, -1, TOP), axis=2
    )
    return dispatch_map, combine_map


def per_device(tokens, expert_ids, gates, w_gate, w_up, w_down):
    n_dp = lax.axis_size("dp")
    n_pipe = lax.axis_size("pipe")
    n_exp = lax.axis_size("expert")
    micro, tok_rows, width = tokens.shape
    units = w_gate.shape[3]
    columns = width // n_dp
    rows_all = n_exp * CAP
    d_me = lax.axis_index("dp")
    p_me = lax.axis_index("pipe")
    e_me = lax.axis_index("expert")
    dring = Ring(n_dp)
    ering = Ring(n_exp)
    small_dp = n_dp <= SMALL_GROUP

    def lin(d, p, e):
        return (d * n_pipe + p) * n_exp + e

    def expert_pairs(p, s, back):
        step = ering.behind if back else ering.ahead
        return [(lin(d, p, e), lin(d, p, step(e, s))) for d in range(n_dp) for e in range(n_exp)]

    def dp_pairs(p, s):
        return [(lin(d, p, e), lin(dring.ahead(d, s), p, e)) for d in range(n_dp) for e in range(n_exp)]

    gate_local = w_gate[0, 0]
    up_local = w_up[0, 0]
    down_local = w_down[0, 0]

    if small_dp:
        down_parts = []
        for s in range(n_dp):
            piece = lax.dynamic_slice_in_dim(down_local, dring.ahead(d_me, s) * columns, columns, 1)
            down_parts.append(piece)
        down_parts, tokens = lax.optimization_barrier((down_parts, tokens))
        for s in range(1, n_dp):
            down_parts[s] = lax.ppermute(down_parts[s], "dp", [(i, dring.ahead(i, s)) for i in range(n_dp)])
        down_full = jnp.concatenate(down_parts, axis=0)
    else:
        down_full = lax.all_to_all(down_local, "dp", 1, 0, tiled=True)

    route_ids = expert_ids[0]
    route_gates = gates[0]
    maps = [build_maps(route_ids[m], route_gates[m], ering, e_me, rows_all) for m in range(micro)]
    dispatch_map = jnp.stack([mp[0] for mp in maps])
    combine_map = jnp.stack([mp[1] for mp in maps])
    absolute_dispatch = dispatch_map
    if ering.xor:
        maps = [build_maps(route_ids[m], route_gates[m], ering, 0, rows_all) for m in range(micro)]
        absolute_dispatch = jnp.stack([mp[0] for mp in maps])
        combine_map = jnp.stack([mp[1] for mp in maps])

    def layer(current, p):
        if p == 0 and ering.xor:
            outgoing = jnp.einsum("mrt,mtd->mrd", absolute_dispatch, current, preferred_element_type=jnp.float32)
            outgoing = outgoing.astype(jnp.bfloat16).reshape(micro, n_exp, CAP, width)
            flat_rows = lax.all_to_all(outgoing, "expert", 1, 1, tiled=True).reshape(-1, width)
            in_block_order = True
        else:
            outgoing = jnp.einsum("mrt,mtd->mrd", dispatch_map, current, preferred_element_type=jnp.float32)
            outgoing = outgoing.astype(jnp.bfloat16).reshape(micro, n_exp, CAP, width)
            arrived = [outgoing[:, 0]]
            for s in range(1, n_exp):
                arrived.append(lax.ppermute(outgoing[:, s], AXES, expert_pairs(p, s, False)))
            flat_rows = jnp.stack(arrived, axis=1).reshape(-1, width)
            in_block_order = False
        squares = jnp.mean(jnp.square(flat_rows.astype(jnp.float32)), axis=1, keepdims=True)
        inv_rms = lax.rsqrt(squares + 1e-05)
        gate_act = jnp.dot(flat_rows, gate_local, preferred_element_type=jnp.float32) * inv_rms
        up_act = jnp.dot(flat_rows, up_local, preferred_element_type=jnp.float32) * inv_rms
        hidden = (jax.nn.silu(gate_act) * up_act).astype(jnp.bfloat16)
        if small_dp:
            parts = [hidden]
            for s in range(1, n_dp):
                parts.append(lax.ppermute(hidden, AXES, dp_pairs(p, s)))
            hidden_full = jnp.concatenate(parts, axis=1)
        else:
            hidden_full = lax.all_gather(hidden, "dp", axis=1, tiled=True)
        expert_out = jnp.dot(hidden_full, down_full, preferred_element_type=jnp.float32).astype(jnp.bfloat16)
        expert_out = expert_out.reshape(micro, n_exp, CAP, columns)
        if ering.xor:
            if in_block_order:
                by_block = expert_out
            else:
                order = jnp.stack([ering.place(j, e_me) for j in range(n_exp)])
                by_block = jnp.take(expert_out, order, axis=1)
            returned = lax.all_to_all(by_block, "expert", 1, 1, tiled=True).reshape(micro, rows_all, columns)
        else:
            returned = [expert_out[:, 0]]
            for s in range(1, n_exp):
                returned.append(lax.ppermute(expert_out[:, s], AXES, expert_pairs(p, s, True)))
            returned = jnp.stack(returned, axis=1).reshape(micro, rows_all, columns)
        mixed = jnp.einsum(
            "mrt,mrc->mtc",
            combine_map,
            returned.astype(jnp.float32),
            precision=lax.Precision.HIGHEST,
            preferred_element_type=jnp.float32,
        )
        current_cols = lax.dynamic_slice_in_dim(current, d_me * columns, columns, 2)
        return (current_cols.astype(jnp.float32) + mixed).astype(jnp.bfloat16)

    current = tokens
    result = None
    for p in range(n_pipe):
        cols = layer(current, p)
        result = cols if result is None else jnp.where(p_me == p, cols, result)
        if p + 1 < n_pipe:
            if small_dp:
                parts = []
                for s in range(n_dp):
                    pairs = [
                        (lin(d, p, e), lin(dring.ahead(d, s), p + 1, e)) for d in range(n_dp) for e in range(n_exp)
                    ]
                    parts.append(lax.ppermute(cols, AXES, pairs))
                stacked = jnp.stack(parts)
                order = jnp.stack([dring.place(d_me, k) for k in range(n_dp)])
                stacked = jnp.take(stacked, order, axis=0)
                current = jnp.transpose(stacked, (1, 2, 0, 3)).reshape(micro, tok_rows, width)
            else:
                full = lax.all_gather(cols, "dp", axis=2, tiled=True)
                current = lax.ppermute(full, "pipe", [(p, p + 1)])
    return result[None]


def solution(mesh):
    return jax.shard_map(
        per_device,
        mesh=mesh,
        in_specs=(
            P(None, "expert", None),
            P("pipe", None, "expert", None),
            P("pipe", None, "expert", None),
            P("pipe", "expert", None, "dp"),
            P("pipe", "expert", None, "dp"),
            P("pipe", "expert", "dp", None),
        ),
        out_specs=P("pipe", None, "expert", "dp"),
        check_vma=False,
    )
```

```python
import jax
import jax.numpy as jnp
from jax import lax
from jax.sharding import PartitionSpec as P

TOP = 2
CAP = 16
AXES = ("dp", "pipe", "expert")
SMALL_GROUP = 8


class Ring:
    def __init__(self, n):
        self.n = n
        self.xor = n & (n - 1) == 0

    def ahead(self, me, s):
        return me ^ s if self.xor else (me + s) % self.n

    def behind(self, me, s):
        return me ^ s if self.xor else (me - s) % self.n

    def place(self, target, me):
        return target ^ me if self.xor else (target - me) % self.n


def build_maps(route_ids, route_gates, ring, me, rows_all):
    experts = ring.n
    flat_ids = route_ids.reshape(-1)
    onehot = (flat_ids[:, None] == jnp.arange(experts, dtype=jnp.int32)[None, :]).astype(jnp.int32)
    before = jnp.cumsum(onehot, axis=0) - onehot
    slot = jnp.sum(before * onehot, axis=1)
    placed = ring.place(flat_ids, me) * CAP + slot
    matches = jnp.arange(rows_all, dtype=jnp.int32)[:, None] == placed[None, :]
    dispatch_map = jnp.sum(matches.astype(jnp.float32).reshape(rows_all, -1, TOP), axis=2).astype(jnp.bfloat16)
    combine_map = jnp.sum(
        jnp.where(matches, route_gates.reshape(-1)[None, :], 0.0).reshape(rows_all, -1, TOP), axis=2
    )
    return dispatch_map, combine_map


def per_device(tokens, expert_ids, gates, w_gate, w_up, w_down):
    n_dp = lax.axis_size("dp")
    n_pipe = lax.axis_size("pipe")
    n_exp = lax.axis_size("expert")
    micro, tok_rows, width = tokens.shape
    units = w_gate.shape[3]
    columns = width // n_dp
    rows_all = n_exp * CAP
    d_me = lax.axis_index("dp")
    p_me = lax.axis_index("pipe")
    e_me = lax.axis_index("expert")
    dring = Ring(n_dp)
    ering = Ring(n_exp)
    small_dp = n_dp <= SMALL_GROUP

    def lin(d, p, e):
        return (d * n_pipe + p) * n_exp + e

    def expert_pairs(p, s, back):
        step = ering.behind if back else ering.ahead
        return [(lin(d, p, e), lin(d, p, step(e, s))) for d in range(n_dp) for e in range(n_exp)]

    def dp_pairs(p, s):
        return [(lin(d, p, e), lin(dring.ahead(d, s), p, e)) for d in range(n_dp) for e in range(n_exp)]

    gate_local = w_gate[0, 0]
    up_local = w_up[0, 0]
    down_local = w_down[0, 0]

    if small_dp:
        down_parts = []
        for s in range(n_dp):
            piece = lax.dynamic_slice_in_dim(down_local, dring.ahead(d_me, s) * columns, columns, 1)
            down_parts.append(piece)
        down_parts, tokens = lax.optimization_barrier((down_parts, tokens))
        for s in range(1, n_dp):
            down_parts[s] = lax.ppermute(down_parts[s], "dp", [(i, dring.ahead(i, s)) for i in range(n_dp)])
        down_full = jnp.concatenate(down_parts, axis=0)
    else:
        down_full = lax.all_to_all(down_local, "dp", 1, 0, tiled=True)

    route_ids = expert_ids[0]
    route_gates = gates[0]
    maps = [build_maps(route_ids[m], route_gates[m], ering, e_me, rows_all) for m in range(micro)]
    dispatch_map = jnp.stack([mp[0] for mp in maps])
    combine_map = jnp.stack([mp[1] for mp in maps])
    if ering.xor:
        combine_map = jnp.stack(
            [build_maps(route_ids[m], route_gates[m], ering, 0, rows_all)[1] for m in range(micro)]
        )

    def layer(current, p):
        outgoing = jnp.einsum("mrt,mtd->mrd", dispatch_map, current, preferred_element_type=jnp.float32)
        outgoing = outgoing.astype(jnp.bfloat16).reshape(micro, n_exp, CAP, width)
        arrived = [outgoing[:, 0]]
        for s in range(1, n_exp):
            arrived.append(lax.ppermute(outgoing[:, s], AXES, expert_pairs(p, s, False)))
        flat_rows = jnp.stack(arrived, axis=1).reshape(-1, width)
        squares = jnp.mean(jnp.square(flat_rows.astype(jnp.float32)), axis=1, keepdims=True)
        inv_rms = lax.rsqrt(squares + 1e-05)
        gate_act = jnp.dot(flat_rows, gate_local, preferred_element_type=jnp.float32) * inv_rms
        up_act = jnp.dot(flat_rows, up_local, preferred_element_type=jnp.float32) * inv_rms
        hidden = (jax.nn.silu(gate_act) * up_act).astype(jnp.bfloat16)
        if small_dp:
            spread = jnp.broadcast_to(hidden[None], (n_dp,) + hidden.shape)
            gathered = lax.all_to_all(spread, "dp", 0, 0, tiled=True)
            order = jnp.stack([dring.behind(d_me, s) for s in range(n_dp)])
            gathered = jnp.take(gathered, order, axis=0)
            hidden_full = jnp.transpose(gathered, (1, 0, 2)).reshape(hidden.shape[0], n_dp * units)
        else:
            hidden_full = lax.all_gather(hidden, "dp", axis=1, tiled=True)
        expert_out = jnp.dot(hidden_full, down_full, preferred_element_type=jnp.float32).astype(jnp.bfloat16)
        expert_out = expert_out.reshape(micro, n_exp, CAP, columns)
        if ering.xor:
            order = jnp.stack([ering.place(j, e_me) for j in range(n_exp)])
            by_block = jnp.take(expert_out, order, axis=1)
            returned = lax.all_to_all(by_block, "expert", 1, 1, tiled=True).reshape(micro, rows_all, columns)
        else:
            returned = [expert_out[:, 0]]
            for s in range(1, n_exp):
                returned.append(lax.ppermute(expert_out[:, s], AXES, expert_pairs(p, s, True)))
            returned = jnp.stack(returned, axis=1).reshape(micro, rows_all, columns)
        mixed = jnp.einsum(
            "mrt,mrc->mtc",
            combine_map,
            returned.astype(jnp.float32),
            precision=lax.Precision.HIGHEST,
            preferred_element_type=jnp.float32,
        )
        current_cols = lax.dynamic_slice_in_dim(current, d_me * columns, columns, 2)
        return (current_cols.astype(jnp.float32) + mixed).astype(jnp.bfloat16)

    current = tokens
    result = None
    for p in range(n_pipe):
        cols = layer(current, p)
        result = cols if result is None else jnp.where(p_me == p, cols, result)
        if p + 1 < n_pipe:
            if small_dp:
                parts = []
                for s in range(n_dp):
                    pairs = [
                        (lin(d, p, e), lin(dring.ahead(d, s), p + 1, e)) for d in range(n_dp) for e in range(n_exp)
                    ]
                    parts.append(lax.ppermute(cols, AXES, pairs))
                stacked = jnp.stack(parts)
                order = jnp.stack([dring.place(d_me, k) for k in range(n_dp)])
                stacked = jnp.take(stacked, order, axis=0)
                current = jnp.transpose(stacked, (1, 2, 0, 3)).reshape(micro, tok_rows, width)
            else:
                full = lax.all_gather(cols, "dp", axis=2, tiled=True)
                current = lax.ppermute(full, "pipe", [(p, p + 1)])
    return result[None]


def solution(mesh):
    return jax.shard_map(
        per_device,
        mesh=mesh,
        in_specs=(
            P(None, "expert", None),
            P("pipe", None, "expert", None),
            P("pipe", None, "expert", None),
            P("pipe", "expert", None, "dp"),
            P("pipe", "expert", None, "dp"),
            P("pipe", "expert", "dp", None),
        ),
        out_specs=P("pipe", None, "expert", "dp"),
        check_vma=False,
    )
```

```python
import jax
import jax.numpy as jnp
from jax import lax
from jax.sharding import PartitionSpec as P

TOP = 2
CAP = 16
AXES = ("dp", "pipe", "expert")
SMALL_GROUP = 8


class Ring:
    def __init__(self, n):
        self.n = n
        self.xor = n & (n - 1) == 0

    def ahead(self, me, s):
        return me ^ s if self.xor else (me + s) % self.n

    def behind(self, me, s):
        return me ^ s if self.xor else (me - s) % self.n

    def place(self, target, me):
        return target ^ me if self.xor else (target - me) % self.n


def build_maps(route_ids, route_gates, ring, me, rows_all):
    experts = ring.n
    flat_ids = route_ids.reshape(-1)
    onehot = (flat_ids[:, None] == jnp.arange(experts, dtype=jnp.int32)[None, :]).astype(jnp.int32)
    before = jnp.cumsum(onehot, axis=0) - onehot
    slot = jnp.sum(before * onehot, axis=1)
    placed = ring.place(flat_ids, me) * CAP + slot
    matches = jnp.arange(rows_all, dtype=jnp.int32)[:, None] == placed[None, :]
    dispatch_map = jnp.sum(matches.astype(jnp.float32).reshape(rows_all, -1, TOP), axis=2).astype(jnp.bfloat16)
    combine_map = jnp.sum(
        jnp.where(matches, route_gates.reshape(-1)[None, :], 0.0).reshape(rows_all, -1, TOP), axis=2
    )
    return dispatch_map, combine_map


def per_device(tokens, expert_ids, gates, w_gate, w_up, w_down):
    n_dp = lax.axis_size("dp")
    n_pipe = lax.axis_size("pipe")
    n_exp = lax.axis_size("expert")
    micro, tok_rows, width = tokens.shape
    units = w_gate.shape[3]
    columns = width // n_dp
    rows_all = n_exp * CAP
    d_me = lax.axis_index("dp")
    p_me = lax.axis_index("pipe")
    e_me = lax.axis_index("expert")
    dring = Ring(n_dp)
    ering = Ring(n_exp)
    small_dp = n_dp <= SMALL_GROUP

    def lin(d, p, e):
        return (d * n_pipe + p) * n_exp + e

    def expert_pairs(p, s, back):
        step = ering.behind if back else ering.ahead
        return [(lin(d, p, e), lin(d, p, step(e, s))) for d in range(n_dp) for e in range(n_exp)]

    def dp_pairs(p, s):
        return [(lin(d, p, e), lin(dring.ahead(d, s), p, e)) for d in range(n_dp) for e in range(n_exp)]

    gate_local = w_gate[0, 0]
    up_local = w_up[0, 0]
    down_local = w_down[0, 0]

    if small_dp:
        down_parts = []
        for s in range(n_dp):
            piece = lax.dynamic_slice_in_dim(down_local, dring.ahead(d_me, s) * columns, columns, 1)
            down_parts.append(piece)
        down_parts, tokens = lax.optimization_barrier((down_parts, tokens))
        for s in range(1, n_dp):
            down_parts[s] = lax.ppermute(down_parts[s], AXES, dp_pairs(0, s))
        down_full = jnp.concatenate(down_parts, axis=0)
    else:
        down_full = lax.all_to_all(down_local, "dp", 1, 0, tiled=True)

    route_ids = expert_ids[0]
    route_gates = gates[0]
    maps = [build_maps(route_ids[m], route_gates[m], ering, e_me, rows_all) for m in range(micro)]
    dispatch_map = jnp.stack([mp[0] for mp in maps])
    combine_map = jnp.stack([mp[1] for mp in maps])
    if ering.xor:
        combine_map = jnp.stack(
            [build_maps(route_ids[m], route_gates[m], ering, 0, rows_all)[1] for m in range(micro)]
        )

    def layer(current, p):
        outgoing = jnp.einsum("mrt,mtd->mrd", dispatch_map, current, preferred_element_type=jnp.float32)
        outgoing = outgoing.astype(jnp.bfloat16).reshape(micro, n_exp, CAP, width)
        arrived = [outgoing[:, 0]]
        for s in range(1, n_exp):
            arrived.append(lax.ppermute(outgoing[:, s], AXES, expert_pairs(p, s, False)))
        flat_rows = jnp.stack(arrived, axis=1).reshape(-1, width)
        squares = jnp.mean(jnp.square(flat_rows.astype(jnp.float32)), axis=1, keepdims=True)
        inv_rms = lax.rsqrt(squares + 1e-05)
        gate_act = jnp.dot(flat_rows, gate_local, preferred_element_type=jnp.float32) * inv_rms
        up_act = jnp.dot(flat_rows, up_local, preferred_element_type=jnp.float32) * inv_rms
        hidden = (jax.nn.silu(gate_act) * up_act).astype(jnp.bfloat16)
        if small_dp and p > 0:
            partial = jnp.dot(hidden, down_local, preferred_element_type=jnp.float32)
            total = lax.dynamic_slice_in_dim(partial, d_me * columns, columns, 1)
            for s in range(1, n_dp):
                chunk = lax.dynamic_slice_in_dim(partial, dring.ahead(d_me, s) * columns, columns, 1)
                total = total + lax.ppermute(chunk.astype(jnp.bfloat16), AXES, dp_pairs(p, s)).astype(jnp.float32)
            expert_out = total.astype(jnp.bfloat16)
        else:
            if small_dp:
                parts = [hidden]
                for s in range(1, n_dp):
                    parts.append(lax.ppermute(hidden, AXES, dp_pairs(p, s)))
                hidden_full = jnp.concatenate(parts, axis=1)
            else:
                hidden_full = lax.all_gather(hidden, "dp", axis=1, tiled=True)
            expert_out = jnp.dot(hidden_full, down_full, preferred_element_type=jnp.float32).astype(jnp.bfloat16)
        expert_out = expert_out.reshape(micro, n_exp, CAP, columns)
        if ering.xor:
            order = jnp.stack([ering.place(j, e_me) for j in range(n_exp)])
            by_block = jnp.take(expert_out, order, axis=1)
            returned = lax.all_to_all(by_block, "expert", 1, 1, tiled=True).reshape(micro, rows_all, columns)
        else:
            returned = [expert_out[:, 0]]
            for s in range(1, n_exp):
                returned.append(lax.ppermute(expert_out[:, s], AXES, expert_pairs(p, s, True)))
            returned = jnp.stack(returned, axis=1).reshape(micro, rows_all, columns)
        mixed = jnp.einsum(
            "mrt,mrc->mtc",
            combine_map,
            returned.astype(jnp.float32),
            precision=lax.Precision.HIGHEST,
            preferred_element_type=jnp.float32,
        )
        current_cols = lax.dynamic_slice_in_dim(current, d_me * columns, columns, 2)
        return (current_cols.astype(jnp.float32) + mixed).astype(jnp.bfloat16)

    current = tokens
    result = None
    for p in range(n_pipe):
        cols = layer(current, p)
        result = cols if result is None else jnp.where(p_me == p, cols, result)
        if p + 1 < n_pipe:
            if small_dp:
                parts = []
                for s in range(n_dp):
                    pairs = [
                        (lin(d, p, e), lin(dring.ahead(d, s), p + 1, e)) for d in range(n_dp) for e in range(n_exp)
                    ]
                    parts.append(lax.ppermute(cols, AXES, pairs))
                stacked = jnp.stack(parts)
                order = jnp.stack([dring.place(d_me, k) for k in range(n_dp)])
                stacked = jnp.take(stacked, order, axis=0)
                current = jnp.transpose(stacked, (1, 2, 0, 3)).reshape(micro, tok_rows, width)
            else:
                full = lax.all_gather(cols, "dp", axis=2, tiled=True)
                current = lax.ppermute(full, "pipe", [(p, p + 1)])
    return result[None]


def solution(mesh):
    return jax.shard_map(
        per_device,
        mesh=mesh,
        in_specs=(
            P(None, "expert", None),
            P("pipe", None, "expert", None),
            P("pipe", None, "expert", None),
            P("pipe", "expert", None, "dp"),
            P("pipe", "expert", None, "dp"),
            P("pipe", "expert", "dp", None),
        ),
        out_specs=P("pipe", None, "expert", "dp"),
        check_vma=False,
    )
```

```python
import jax
import jax.numpy as jnp
from jax import lax
from jax.sharding import PartitionSpec as P

TOP = 2
CAP = 16
AXES = ("dp", "pipe", "expert")
SMALL_GROUP = 8


class Ring:
    def __init__(self, n):
        self.n = n
        self.xor = n & (n - 1) == 0

    def ahead(self, me, s):
        return me ^ s if self.xor else (me + s) % self.n

    def behind(self, me, s):
        return me ^ s if self.xor else (me - s) % self.n

    def place(self, target, me):
        return target ^ me if self.xor else (target - me) % self.n


def build_maps(route_ids, route_gates, ring, me, rows_all):
    experts = ring.n
    flat_ids = route_ids.reshape(-1)
    onehot = (flat_ids[:, None] == jnp.arange(experts, dtype=jnp.int32)[None, :]).astype(jnp.int32)
    before = jnp.cumsum(onehot, axis=0) - onehot
    slot = jnp.sum(before * onehot, axis=1)
    placed = ring.place(flat_ids, me) * CAP + slot
    matches = jnp.arange(rows_all, dtype=jnp.int32)[:, None] == placed[None, :]
    dispatch_map = jnp.sum(matches.astype(jnp.float32).reshape(rows_all, -1, TOP), axis=2).astype(jnp.bfloat16)
    combine_map = jnp.sum(
        jnp.where(matches, route_gates.reshape(-1)[None, :], 0.0).reshape(rows_all, -1, TOP), axis=2
    )
    return dispatch_map, combine_map


def per_device(tokens, expert_ids, gates, w_gate, w_up, w_down):
    n_dp = lax.axis_size("dp")
    n_pipe = lax.axis_size("pipe")
    n_exp = lax.axis_size("expert")
    micro, tok_rows, width = tokens.shape
    units = w_gate.shape[3]
    columns = width // n_dp
    rows_all = n_exp * CAP
    d_me = lax.axis_index("dp")
    p_me = lax.axis_index("pipe")
    e_me = lax.axis_index("expert")
    dring = Ring(n_dp)
    ering = Ring(n_exp)
    small_dp = n_dp <= SMALL_GROUP

    def lin(d, p, e):
        return (d * n_pipe + p) * n_exp + e

    def expert_pairs(p, s, back):
        step = ering.behind if back else ering.ahead
        return [(lin(d, p, e), lin(d, p, step(e, s))) for d in range(n_dp) for e in range(n_exp)]

    def dp_pairs(p, s):
        return [(lin(d, p, e), lin(dring.ahead(d, s), p, e)) for d in range(n_dp) for e in range(n_exp)]

    gate_local = w_gate[0, 0]
    up_local = w_up[0, 0]
    down_local = w_down[0, 0]

    if small_dp:
        down_parts = []
        for s in range(n_dp):
            piece = lax.dynamic_slice_in_dim(down_local, dring.ahead(d_me, s) * columns, columns, 1)
            down_parts.append(piece)
        down_parts, tokens = lax.optimization_barrier((down_parts, tokens))
        for s in range(1, n_dp):
            down_parts[s] = lax.ppermute(down_parts[s], "dp", [(i, dring.ahead(i, s)) for i in range(n_dp)])
        down_full = jnp.concatenate(down_parts, axis=0)
    else:
        down_full = lax.all_to_all(down_local, "dp", 1, 0, tiled=True)

    route_ids = expert_ids[0]
    route_gates = gates[0]
    maps = [build_maps(route_ids[m], route_gates[m], ering, e_me, rows_all) for m in range(micro)]
    dispatch_map = jnp.stack([mp[0] for mp in maps])
    combine_map = jnp.stack([mp[1] for mp in maps])
    if ering.xor:
        combine_map = jnp.stack(
            [build_maps(route_ids[m], route_gates[m], ering, 0, rows_all)[1] for m in range(micro)]
        )

    def layer(current, p):
        outgoing = jnp.einsum("mrt,mtd->mrd", dispatch_map, current, preferred_element_type=jnp.float32)
        outgoing = outgoing.astype(jnp.bfloat16).reshape(micro, n_exp, CAP, width)
        arrived = [outgoing[:, 0]]
        for s in range(1, n_exp):
            arrived.append(lax.ppermute(outgoing[:, s], AXES, expert_pairs(p, s, False)))
        flat_rows = jnp.stack(arrived, axis=1).reshape(-1, width)
        squares = jnp.mean(jnp.square(flat_rows.astype(jnp.float32)), axis=1, keepdims=True)
        inv_rms = lax.rsqrt(squares + 1e-05)
        gate_act = jnp.dot(flat_rows, gate_local, preferred_element_type=jnp.float32) * inv_rms
        up_act = jnp.dot(flat_rows, up_local, preferred_element_type=jnp.float32) * inv_rms
        hidden = (jax.nn.silu(gate_act) * up_act).astype(jnp.bfloat16)
        if small_dp and p == 0:
            spread = jnp.broadcast_to(hidden[None], (n_dp,) + hidden.shape)
            gathered = lax.all_to_all(spread, "dp", 0, 0, tiled=True)
            order = jnp.stack([dring.behind(d_me, s) for s in range(n_dp)])
            gathered = jnp.take(gathered, order, axis=0)
            hidden_full = jnp.transpose(gathered, (1, 0, 2)).reshape(hidden.shape[0], n_dp * units)
        elif small_dp:
            parts = [hidden]
            for s in range(1, n_dp):
                parts.append(lax.ppermute(hidden, AXES, dp_pairs(p, s)))
            hidden_full = jnp.concatenate(parts, axis=1)
        else:
            hidden_full = lax.all_gather(hidden, "dp", axis=1, tiled=True)
        expert_out = jnp.dot(hidden_full, down_full, preferred_element_type=jnp.float32).astype(jnp.bfloat16)
        expert_out = expert_out.reshape(micro, n_exp, CAP, columns)
        if ering.xor:
            order = jnp.stack([ering.place(j, e_me) for j in range(n_exp)])
            by_block = jnp.take(expert_out, order, axis=1)
            returned = lax.all_to_all(by_block, "expert", 1, 1, tiled=True).reshape(micro, rows_all, columns)
        else:
            returned = [expert_out[:, 0]]
            for s in range(1, n_exp):
                returned.append(lax.ppermute(expert_out[:, s], AXES, expert_pairs(p, s, True)))
            returned = jnp.stack(returned, axis=1).reshape(micro, rows_all, columns)
        mixed = jnp.einsum(
            "mrt,mrc->mtc",
            combine_map,
            returned.astype(jnp.float32),
            precision=lax.Precision.HIGHEST,
            preferred_element_type=jnp.float32,
        )
        current_cols = lax.dynamic_slice_in_dim(current, d_me * columns, columns, 2)
        return (current_cols.astype(jnp.float32) + mixed).astype(jnp.bfloat16)

    current = tokens
    result = None
    for p in range(n_pipe):
        cols = layer(current, p)
        result = cols if result is None else jnp.where(p_me == p, cols, result)
        if p + 1 < n_pipe:
            if small_dp:
                parts = []
                for s in range(n_dp):
                    pairs = [
                        (lin(d, p, e), lin(dring.ahead(d, s), p + 1, e)) for d in range(n_dp) for e in range(n_exp)
                    ]
                    parts.append(lax.ppermute(cols, AXES, pairs))
                stacked = jnp.stack(parts)
                order = jnp.stack([dring.place(d_me, k) for k in range(n_dp)])
                stacked = jnp.take(stacked, order, axis=0)
                current = jnp.transpose(stacked, (1, 2, 0, 3)).reshape(micro, tok_rows, width)
            else:
                full = lax.all_gather(cols, "dp", axis=2, tiled=True)
                current = lax.ppermute(full, "pipe", [(p, p + 1)])
    return result[None]


def solution(mesh):
    return jax.shard_map(
        per_device,
        mesh=mesh,
        in_specs=(
            P(None, "expert", None),
            P("pipe", None, "expert", None),
            P("pipe", None, "expert", None),
            P("pipe", "expert", None, "dp"),
            P("pipe", "expert", None, "dp"),
            P("pipe", "expert", "dp", None),
        ),
        out_specs=P("pipe", None, "expert", "dp"),
        check_vma=False,
    )
```

```python
import jax
import jax.numpy as jnp
from jax import lax
from jax.sharding import PartitionSpec as P

TOP = 2
CAP = 16
AXES = ("dp", "pipe", "expert")
SMALL_GROUP = 8


class Ring:
    def __init__(self, n):
        self.n = n
        self.xor = n & (n - 1) == 0

    def ahead(self, me, s):
        return me ^ s if self.xor else (me + s) % self.n

    def behind(self, me, s):
        return me ^ s if self.xor else (me - s) % self.n

    def place(self, target, me):
        return target ^ me if self.xor else (target - me) % self.n


def build_maps(route_ids, route_gates, ring, me, rows_all):
    experts = ring.n
    flat_ids = route_ids.reshape(-1)
    onehot = (flat_ids[:, None] == jnp.arange(experts, dtype=jnp.int32)[None, :]).astype(jnp.int32)
    before = jnp.cumsum(onehot, axis=0) - onehot
    slot = jnp.sum(before * onehot, axis=1)
    placed = ring.place(flat_ids, me) * CAP + slot
    matches = jnp.arange(rows_all, dtype=jnp.int32)[:, None] == placed[None, :]
    dispatch_map = jnp.sum(matches.astype(jnp.float32).reshape(rows_all, -1, TOP), axis=2).astype(jnp.bfloat16)
    combine_map = jnp.sum(
        jnp.where(matches, route_gates.reshape(-1)[None, :], 0.0).reshape(rows_all, -1, TOP), axis=2
    )
    return dispatch_map, combine_map


def per_device(tokens, expert_ids, gates, w_gate, w_up, w_down):
    n_dp = lax.axis_size("dp")
    n_pipe = lax.axis_size("pipe")
    n_exp = lax.axis_size("expert")
    micro, tok_rows, width = tokens.shape
    units = w_gate.shape[3]
    columns = width // n_dp
    rows_all = n_exp * CAP
    d_me = lax.axis_index("dp")
    p_me = lax.axis_index("pipe")
    e_me = lax.axis_index("expert")
    dring = Ring(n_dp)
    ering = Ring(n_exp)
    small_dp = n_dp <= SMALL_GROUP

    def lin(d, p, e):
        return (d * n_pipe + p) * n_exp + e

    def expert_pairs(p, s, back):
        step = ering.behind if back else ering.ahead
        return [(lin(d, p, e), lin(d, p, step(e, s))) for d in range(n_dp) for e in range(n_exp)]

    def dp_pairs(p, s):
        return [(lin(d, p, e), lin(dring.ahead(d, s), p, e)) for d in range(n_dp) for e in range(n_exp)]

    gate_local = w_gate[0, 0]
    up_local = w_up[0, 0]
    down_local = w_down[0, 0]

    if small_dp:
        down_parts = []
        for s in range(n_dp):
            piece = lax.dynamic_slice_in_dim(down_local, dring.ahead(d_me, s) * columns, columns, 1)
            down_parts.append(piece)
        down_parts, tokens = lax.optimization_barrier((down_parts, tokens))
        for s in range(1, n_dp):
            down_parts[s] = lax.ppermute(down_parts[s], "dp", [(i, dring.ahead(i, s)) for i in range(n_dp)])
        down_full = jnp.concatenate(down_parts, axis=0)
    else:
        down_full = lax.all_to_all(down_local, "dp", 1, 0, tiled=True)

    route_ids = expert_ids[0]
    route_gates = gates[0]
    maps = [build_maps(route_ids[m], route_gates[m], ering, e_me, rows_all) for m in range(micro)]
    dispatch_map = jnp.stack([mp[0] for mp in maps])
    combine_map = jnp.stack([mp[1] for mp in maps])
    if ering.xor:
        flat_ids = route_ids.reshape(micro, -1)
        onehot = (flat_ids[:, :, None] == jnp.arange(n_exp, dtype=jnp.int32)).astype(jnp.int32)
        before = jnp.cumsum(onehot, axis=1) - onehot
        pair_rows = flat_ids * CAP + jnp.sum(before * onehot, axis=2)

    def layer(current, p):
        outgoing = jnp.einsum("mrt,mtd->mrd", dispatch_map, current, preferred_element_type=jnp.float32)
        outgoing = outgoing.astype(jnp.bfloat16).reshape(micro, n_exp, CAP, width)
        arrived = [outgoing[:, 0]]
        for s in range(1, n_exp):
            arrived.append(lax.ppermute(outgoing[:, s], AXES, expert_pairs(p, s, False)))
        flat_rows = jnp.stack(arrived, axis=1).reshape(-1, width)
        squares = jnp.mean(jnp.square(flat_rows.astype(jnp.float32)), axis=1, keepdims=True)
        inv_rms = lax.rsqrt(squares + 1e-05)
        gate_act = jnp.dot(flat_rows, gate_local, preferred_element_type=jnp.float32) * inv_rms
        up_act = jnp.dot(flat_rows, up_local, preferred_element_type=jnp.float32) * inv_rms
        hidden = (jax.nn.silu(gate_act) * up_act).astype(jnp.bfloat16)
        if small_dp:
            parts = [hidden]
            for s in range(1, n_dp):
                parts.append(lax.ppermute(hidden, AXES, dp_pairs(p, s)))
            hidden_full = jnp.concatenate(parts, axis=1)
        else:
            hidden_full = lax.all_gather(hidden, "dp", axis=1, tiled=True)
        expert_out = jnp.dot(hidden_full, down_full, preferred_element_type=jnp.float32).astype(jnp.bfloat16)
        expert_out = expert_out.reshape(micro, n_exp, CAP, columns)
        if ering.xor:
            order = jnp.stack([ering.place(j, e_me) for j in range(n_exp)])
            by_block = jnp.take(expert_out, order, axis=1)
            returned = lax.all_to_all(by_block, "expert", 1, 1, tiled=True).reshape(micro, rows_all, columns)
        else:
            returned = [expert_out[:, 0]]
            for s in range(1, n_exp):
                returned.append(lax.ppermute(expert_out[:, s], AXES, expert_pairs(p, s, True)))
            returned = jnp.stack(returned, axis=1).reshape(micro, rows_all, columns)
        if ering.xor:
            picked = jnp.take_along_axis(returned, pair_rows[:, :, None], axis=1).astype(jnp.float32)
            picked = picked.reshape(micro, tok_rows, TOP, columns)
            mixed = jnp.sum(route_gates[:, :, :, None] * picked, axis=2)
        else:
            mixed = jnp.einsum(
                "mrt,mrc->mtc",
                combine_map,
                returned.astype(jnp.float32),
                precision=lax.Precision.HIGHEST,
                preferred_element_type=jnp.float32,
            )
        current_cols = lax.dynamic_slice_in_dim(current, d_me * columns, columns, 2)
        return (current_cols.astype(jnp.float32) + mixed).astype(jnp.bfloat16)

    current = tokens
    result = None
    for p in range(n_pipe):
        cols = layer(current, p)
        result = cols if result is None else jnp.where(p_me == p, cols, result)
        if p + 1 < n_pipe:
            if small_dp:
                parts = []
                for s in range(n_dp):
                    pairs = [
                        (lin(d, p, e), lin(dring.ahead(d, s), p + 1, e)) for d in range(n_dp) for e in range(n_exp)
                    ]
                    parts.append(lax.ppermute(cols, AXES, pairs))
                stacked = jnp.stack(parts)
                order = jnp.stack([dring.place(d_me, k) for k in range(n_dp)])
                stacked = jnp.take(stacked, order, axis=0)
                current = jnp.transpose(stacked, (1, 2, 0, 3)).reshape(micro, tok_rows, width)
            else:
                full = lax.all_gather(cols, "dp", axis=2, tiled=True)
                current = lax.ppermute(full, "pipe", [(p, p + 1)])
    return result[None]


def solution(mesh):
    return jax.shard_map(
        per_device,
        mesh=mesh,
        in_specs=(
            P(None, "expert", None),
            P("pipe", None, "expert", None),
            P("pipe", None, "expert", None),
            P("pipe", "expert", None, "dp"),
            P("pipe", "expert", None, "dp"),
            P("pipe", "expert", "dp", None),
        ),
        out_specs=P("pipe", None, "expert", "dp"),
        check_vma=False,
    )
```

```python
import jax
import jax.numpy as jnp
from jax import lax
from jax.sharding import PartitionSpec as P

TOP = 2
CAP = 16
AXES = ("dp", "pipe", "expert")
SMALL_GROUP = 8


class Ring:
    def __init__(self, n):
        self.n = n
        self.xor = n & (n - 1) == 0

    def ahead(self, me, s):
        return me ^ s if self.xor else (me + s) % self.n

    def behind(self, me, s):
        return me ^ s if self.xor else (me - s) % self.n

    def place(self, target, me):
        return target ^ me if self.xor else (target - me) % self.n


def build_maps(route_ids, route_gates, ring, me, rows_all):
    experts = ring.n
    flat_ids = route_ids.reshape(-1)
    onehot = (flat_ids[:, None] == jnp.arange(experts, dtype=jnp.int32)[None, :]).astype(jnp.int32)
    before = jnp.cumsum(onehot, axis=0) - onehot
    slot = jnp.sum(before * onehot, axis=1)
    placed = ring.place(flat_ids, me) * CAP + slot
    matches = jnp.arange(rows_all, dtype=jnp.int32)[:, None] == placed[None, :]
    dispatch_map = jnp.sum(matches.astype(jnp.float32).reshape(rows_all, -1, TOP), axis=2).astype(jnp.bfloat16)
    combine_map = jnp.sum(
        jnp.where(matches, route_gates.reshape(-1)[None, :], 0.0).reshape(rows_all, -1, TOP), axis=2
    )
    return dispatch_map, combine_map


def per_device(tokens, expert_ids, gates, w_gate, w_up, w_down):
    n_dp = lax.axis_size("dp")
    n_pipe = lax.axis_size("pipe")
    n_exp = lax.axis_size("expert")
    micro, tok_rows, width = tokens.shape
    units = w_gate.shape[3]
    columns = width // n_dp
    rows_all = n_exp * CAP
    d_me = lax.axis_index("dp")
    p_me = lax.axis_index("pipe")
    e_me = lax.axis_index("expert")
    dring = Ring(n_dp)
    ering = Ring(n_exp)
    small_dp = n_dp <= SMALL_GROUP

    def lin(d, p, e):
        return (d * n_pipe + p) * n_exp + e

    def expert_pairs(p, s, back):
        step = ering.behind if back else ering.ahead
        return [(lin(d, p, e), lin(d, p, step(e, s))) for d in range(n_dp) for e in range(n_exp)]

    def dp_pairs(p, s):
        return [(lin(d, p, e), lin(dring.ahead(d, s), p, e)) for d in range(n_dp) for e in range(n_exp)]

    gate_local = w_gate[0, 0]
    up_local = w_up[0, 0]
    down_local = w_down[0, 0]

    if small_dp:
        down_parts = []
        for s in range(n_dp):
            piece = lax.dynamic_slice_in_dim(down_local, dring.ahead(d_me, s) * columns, columns, 1)
            down_parts.append(piece)
        down_parts, tokens = lax.optimization_barrier((down_parts, tokens))
        for s in range(1, n_dp):
            down_parts[s] = lax.ppermute(down_parts[s], "dp", [(i, dring.ahead(i, s)) for i in range(n_dp)])
        down_full = jnp.concatenate(down_parts, axis=0)
    else:
        down_full = lax.all_to_all(down_local, "dp", 1, 0, tiled=True)

    route_ids = expert_ids[0]
    route_gates = gates[0]
    maps = [build_maps(route_ids[m], route_gates[m], ering, e_me, rows_all) for m in range(micro)]
    dispatch_map = jnp.stack([mp[0] for mp in maps])
    combine_map = jnp.stack([mp[1] for mp in maps])
    if ering.xor:
        combine_map = jnp.stack(
            [build_maps(route_ids[m], route_gates[m], ering, 0, rows_all)[1] for m in range(micro)]
        )

    gates_high = combine_map.astype(jnp.bfloat16)
    gates_low = (combine_map - gates_high.astype(jnp.float32)).astype(jnp.bfloat16)

    def layer(current, p):
        outgoing = jnp.einsum("mrt,mtd->mrd", dispatch_map, current, preferred_element_type=jnp.float32)
        outgoing = outgoing.astype(jnp.bfloat16).reshape(micro, n_exp, CAP, width)
        arrived = [outgoing[:, 0]]
        for s in range(1, n_exp):
            arrived.append(lax.ppermute(outgoing[:, s], AXES, expert_pairs(p, s, False)))
        flat_rows = jnp.stack(arrived, axis=1).reshape(-1, width)
        squares = jnp.mean(jnp.square(flat_rows.astype(jnp.float32)), axis=1, keepdims=True)
        inv_rms = lax.rsqrt(squares + 1e-05)
        gate_act = jnp.dot(flat_rows, gate_local, preferred_element_type=jnp.float32) * inv_rms
        up_act = jnp.dot(flat_rows, up_local, preferred_element_type=jnp.float32) * inv_rms
        hidden = (jax.nn.silu(gate_act) * up_act).astype(jnp.bfloat16)
        if small_dp:
            parts = [hidden]
            for s in range(1, n_dp):
                parts.append(lax.ppermute(hidden, AXES, dp_pairs(p, s)))
            hidden_full = jnp.concatenate(parts, axis=1)
        else:
            hidden_full = lax.all_gather(hidden, "dp", axis=1, tiled=True)
        expert_out = jnp.dot(hidden_full, down_full, preferred_element_type=jnp.float32).astype(jnp.bfloat16)
        expert_out = expert_out.reshape(micro, n_exp, CAP, columns)
        if ering.xor:
            order = jnp.stack([ering.place(j, e_me) for j in range(n_exp)])
            by_block = jnp.take(expert_out, order, axis=1)
            returned = lax.all_to_all(by_block, "expert", 1, 1, tiled=True).reshape(micro, rows_all, columns)
        else:
            returned = [expert_out[:, 0]]
            for s in range(1, n_exp):
                returned.append(lax.ppermute(expert_out[:, s], AXES, expert_pairs(p, s, True)))
            returned = jnp.stack(returned, axis=1).reshape(micro, rows_all, columns)
        mixed = jnp.einsum("mrt,mrc->mtc", gates_high, returned, preferred_element_type=jnp.float32)
        mixed = mixed + jnp.einsum("mrt,mrc->mtc", gates_low, returned, preferred_element_type=jnp.float32)
        current_cols = lax.dynamic_slice_in_dim(current, d_me * columns, columns, 2)
        return (current_cols.astype(jnp.float32) + mixed).astype(jnp.bfloat16)

    current = tokens
    result = None
    for p in range(n_pipe):
        cols = layer(current, p)
        result = cols if result is None else jnp.where(p_me == p, cols, result)
        if p + 1 < n_pipe:
            if small_dp:
                parts = []
                for s in range(n_dp):
                    pairs = [
                        (lin(d, p, e), lin(dring.ahead(d, s), p + 1, e)) for d in range(n_dp) for e in range(n_exp)
                    ]
                    parts.append(lax.ppermute(cols, AXES, pairs))
                stacked = jnp.stack(parts)
                order = jnp.stack([dring.place(d_me, k) for k in range(n_dp)])
                stacked = jnp.take(stacked, order, axis=0)
                current = jnp.transpose(stacked, (1, 2, 0, 3)).reshape(micro, tok_rows, width)
            else:
                full = lax.all_gather(cols, "dp", axis=2, tiled=True)
                current = lax.ppermute(full, "pipe", [(p, p + 1)])
    return result[None]


def solution(mesh):
    return jax.shard_map(
        per_device,
        mesh=mesh,
        in_specs=(
            P(None, "expert", None),
            P("pipe", None, "expert", None),
            P("pipe", None, "expert", None),
            P("pipe", "expert", None, "dp"),
            P("pipe", "expert", None, "dp"),
            P("pipe", "expert", "dp", None),
        ),
        out_specs=P("pipe", None, "expert", "dp"),
        check_vma=False,
    )
```
